128 devices in a mesh: wide: 16 (over x, y_hi, core), narrow: 8 (over z, y_lo).
Axes of the slice: x: 4, y: 4 (y_hi: 2, y_lo: 2; y = y_hi * 2 + y_lo), z: 4, core: 2. Of those that a mesh axis runs over, the one named last changes fastest.
Arguments:
- hidden_in: bfloat16 [128, 8192], P('narrow', 'wide'), may hold values from -75 to 75
- lengths: int32 [128], P('wide'), may hold values from 32 to 8192, as said below
- kv_cache: bfloat16 [2, 2, 152576, 1024], P(None, None, 'wide', 'narrow'), may hold values from -210 to 210, as said below
- qkv_weight: bfloat16 [8192, 8, 1280], P('wide', 'narrow'), may hold values from -0.0625 to 0.0625
- o_weight: bfloat16 [8192, 8192], P('narrow', 'wide'), may hold values from -0.0625 to 0.0625
- gate_up: bfloat16 [8192, 2, 28672], P('wide', None, 'narrow'), may hold values from -0.0625 to 0.0625
- down_weight: bfloat16 [28672, 8192], P('narrow', 'wide'), may hold values from -0.03125 to 0.03125
- attn_gain: bfloat16 [8192], P('wide'), may hold values from 0.099609375 to 1.8984375
- mlp_gain: bfloat16 [8192], P('wide'), may hold values from 0.099609375 to 1.8984375
Outputs:
- hidden_out: bfloat16 [128, 8192], P('narrow', 'wide')
- new_entries: bfloat16 [2, 2, 128, 1024], P(None, None, 'wide', 'narrow')
The draws below stay inside these ranges and needn't reach their ends.
Inputs may be any that keep to these rules, and one draw needn't show every extreme that they name: Exactly 8 requests have 8192 cached tokens, no two in the same aligned block of 8 requests; every other request has 32 to 192. The lengths of each aligned block of 8 requests sum to at most 9536, and those of one block to exactly 9536. `kv_cache`: cache positions that no request owns hold no live entries.
All inputs are finite; a program needn't handle non-finite values.
Results may differ from the reference program's by a relative error of at most 0.017.
Values may be sent and summed in bfloat16 or wider, within the bound.
No kernel may reach another device: no remote copies, remote signals or barrier semaphores. Data moves between devices by JAX's collectives and lax.ppermute only.
A program may use at most 128 MiB of HBM per device.

```python
import math
import jax
import jax.numpy as jnp
from jax import lax

D = 8192
HQ = 64
KVH = 8
HD = 128
FF = 28672
GROUP = 8
QKV_COLS = 1280
LAYERS = 2
REQ_DEV = 8
REQUESTS = 128
LONG = 8192
SHORT_MIN = 32
SHORT_MAX = 192
LONG_COUNT = 8
CACHE_TOK = 9536
CACHE_ALL = 152576


def draw_hidden_in(key, part):
    key_list = jax.random.split(key, 3)
    col_level = jax.random.uniform(key_list[0], (1, D), jnp.float32)
    row_level = jax.random.uniform(key_list[1], (REQUESTS, 1), jnp.float32)
    rising = jnp.exp(jnp.log(3.0) * (jnp.arange(D, dtype=jnp.float32)[None, :] / D - 0.5))
    base_draw = jnp.clip(jax.random.normal(key_list[2], (REQUESTS, D), jnp.float32), -4.0, 4.0)
    row_scale = jnp.exp(jnp.log(10.0) * (row_level - 0.5))
    col_scale = jnp.exp(jnp.log(10.0) * (col_level - 0.5)) * rising
    return (base_draw * row_scale * col_scale).astype(jnp.bfloat16)


def draw_lengths(key, part):
    key_list = jax.random.split(key, 3)
    blocks = REQUESTS // REQ_DEV
    short_len = jax.random.randint(key_list[0], (blocks, REQ_DEV), SHORT_MIN, SHORT_MAX + 1)
    chosen = jax.random.permutation(key_list[1], blocks)[:LONG_COUNT]
    slot_pick = jax.random.randint(key_list[2], (LONG_COUNT,), 0, REQ_DEV)
    block_ids = jnp.arange(blocks, dtype=jnp.int32)
    slot_ids = jnp.arange(REQ_DEV, dtype=jnp.int32)
    filled = (block_ids == chosen[0])[:, None]
    short_len = jnp.where(filled, SHORT_MAX, short_len)
    is_long = jnp.any((block_ids[None, :, None] == chosen[:, None, None]) & (slot_ids[None, None, :] == slot_pick[:, None, None]), axis=0)
    return jnp.where(is_long, LONG, short_len).reshape(REQUESTS).astype(jnp.int32)


def draw_kv_cache(key, part):
    key_list = jax.random.split(key, 2)
    half_shape = (LAYERS, 1, CACHE_ALL, KVH * HD)
    value_part = jnp.clip(jax.random.normal(key_list[0], half_shape, jnp.float32), -4.0, 4.0)
    key_part = jnp.clip(jax.random.normal(key_list[1], half_shape, jnp.float32), -4.0, 4.0)
    return jnp.concatenate([key_part, value_part], axis=1).astype(jnp.bfloat16)


def block_scale(rng, shape, shards, low, largest):
    level, own = 1.0, jax.random.fold_in(rng, 6)
    for dim, shards_of in shards:
        draws = jnp.exp(jax.random.uniform(jax.random.fold_in(own, dim), (shards_of,), jnp.float32, low / len(shards), largest / len(shards)))
        level = level * jnp.repeat(draws, shape[dim] // shards_of).reshape([-1 if axis == dim else 1 for axis in range(len(shape))])
    return level


def scatter_about(key, shape, scale, limit, cuts=(), kind=jnp.bfloat16):
    level = block_scale(key, shape, cuts, -0.22, 0.18) if cuts else 1.0
    values = jax.random.normal(key, shape, jnp.float32) * scale * level
    return jnp.minimum(jnp.maximum(values, -limit), limit).astype(kind)


def setup_inputs(seed: int = 0) -> dict:
    key_of = jax.random.split(jax.random.key(seed), 10)
    hidden_in = draw_hidden_in(jax.random.fold_in(key_of[9], 71), 0)
    lengths = draw_lengths(jax.random.fold_in(key_of[9], 71), 0)
    kv_cache = draw_kv_cache(jax.random.fold_in(key_of[9], 71), 0)
    qkv_weight = scatter_about(key_of[3], (D, KVH, QKV_COLS), D ** -0.5, 0.0625, ((0, 16), (1, 8)))
    o_weight = scatter_about(key_of[4], (HQ * HD, D), (HQ * HD) ** -0.5, 0.0625, ((0, 8), (1, 16)))
    gate_up = scatter_about(key_of[5], (D, 2, FF), D ** -0.5, 0.0625, ((0, 16), (2, 8)))
    down_weight = scatter_about(key_of[6], (FF, D), FF ** -0.5, 0.03125, ((0, 8), (1, 16)))
    attn_gain = jnp.clip(1.0 + 0.18 * jax.random.normal(key_of[7], (D,), jnp.float32), 0.099609375, 1.8984375).astype(jnp.bfloat16)
    mlp_gain = jnp.clip(1.0 + 0.18 * jax.random.normal(key_of[8], (D,), jnp.float32), 0.099609375, 1.8984375).astype(jnp.bfloat16)
    return {"hidden_in": hidden_in, "lengths": lengths, "kv_cache": kv_cache, "qkv_weight": qkv_weight, "o_weight": o_weight, "gate_up": gate_up, "down_weight": down_weight, "attn_gain": attn_gain, "mlp_gain": mlp_gain}


EPSILON = 1e-05
ROPE_BASE = 500000.0

def rms_norm(stream, gain):
    floats = stream.astype(jnp.float32)
    square_sum = lax.optimization_barrier(jnp.sum(floats * floats, axis=1))
    scaled = floats * lax.rsqrt(square_sum / D + EPSILON)[:, None] * gain.astype(jnp.float32)[None, :]
    return scaled.astype(jnp.bfloat16)

def rotate_pairs(vectors, cosine, sine_table):
    half_dim = vectors.shape[-1] // 2
    first_half = vectors[..., :half_dim]
    second_half = vectors[..., half_dim:]
    return jnp.concatenate([first_half * cosine - second_half * sine_table, second_half * cosine + first_half * sine_table], axis=-1)

def rotary_tables(lengths, head_dim):
    half_dim = head_dim // 2
    inverse = jnp.exp(jnp.arange(half_dim, dtype=jnp.float32) * (-2.0 * math.log(ROPE_BASE) / head_dim))
    angles = lengths.astype(jnp.float32)[:, None] * inverse[None, :]
    return (jnp.cos(angles), jnp.sin(angles))

def split_heads(projected, lengths, heads_kv, head_dim):
    row_count = projected.shape[0]
    grouped = projected.reshape(row_count, heads_kv, -1, head_dim)
    group_size = grouped.shape[2] - 2
    cosine, sine_table = rotary_tables(lengths, head_dim)
    rotated = rotate_pairs(grouped[:, :, :group_size + 1], cosine[:, None, None, :], sine_table[:, None, None, :])
    queries = rotated[:, :, :group_size].astype(jnp.bfloat16)
    key_new = rotated[:, :, group_size].astype(jnp.bfloat16)
    value_new = grouped[:, :, group_size + 1].astype(jnp.bfloat16)
    return (queries, key_new, value_new)

def attend(queries, key_new, value_new, cached_keys, cached_values, lengths):
    row_count, heads_kv, group_size, head_dim = queries.shape
    slot_count = cached_keys.shape[0]
    score_scale = 1.0 / math.sqrt(head_dim)
    key_table = cached_keys.reshape(slot_count, heads_kv, head_dim).astype(jnp.float32)
    value_table = cached_values.reshape(slot_count, heads_kv, head_dim).astype(jnp.float32)
    starts = jnp.cumsum(lengths) - lengths
    position = jnp.arange(slot_count, dtype=jnp.int32)
    owned = (position[None, :] >= starts[:, None]) & (position[None, :] < (starts + lengths)[:, None])
    query_floats = queries.astype(jnp.float32)
    scores = jnp.einsum('rkgd,tkd->krgt', query_floats, key_table, precision=lax.Precision.HIGHEST) * score_scale
    scores = jnp.where(owned[None, :, None, :], scores, -jnp.inf)
    own_score = jnp.einsum('rkgd,rkd->krg', query_floats, key_new.astype(jnp.float32), precision=lax.Precision.HIGHEST) * score_scale
    row_peak = jnp.maximum(lax.optimization_barrier(jnp.max(scores, axis=3)), own_score)
    weights = jnp.exp(scores - row_peak[..., None])
    own_weight = jnp.exp(own_score - row_peak)
    weight_sum = lax.optimization_barrier(jnp.sum(weights, axis=3)) + own_weight
    weights_rounded = lax.optimization_barrier(weights.astype(jnp.bfloat16)).astype(jnp.float32)
    blended = jnp.einsum('krgt,tkd->krgd', weights_rounded, value_table, precision=lax.Precision.HIGHEST)
    own_rounded = lax.optimization_barrier(own_weight.astype(jnp.bfloat16)).astype(jnp.float32)
    blended = blended + own_rounded[..., None] * jnp.transpose(value_new, (1, 0, 2))[:, :, None, :].astype(jnp.float32)
    normalized = (blended / weight_sum[..., None]).astype(jnp.bfloat16)
    return jnp.transpose(normalized, (1, 0, 2, 3)).reshape(row_count, heads_kv * group_size * head_dim)

def attend_item(item_tuple):
    queries, key_new, value_new, cached_keys, cached_values, lengths = item_tuple
    return attend(queries, key_new, value_new, cached_keys, cached_values, lengths)

def reference(hidden_in, lengths, kv_cache, qkv_weight, o_weight, gate_up, down_weight, attn_gain, mlp_gain):
    blocks = REQUESTS // REQ_DEV
    stream = hidden_in
    entries = []
    for layer_index in range(LAYERS):
        normed = rms_norm(stream, attn_gain)
        projected = jnp.dot(normed, qkv_weight.reshape(D, KVH * QKV_COLS), preferred_element_type=jnp.float32)
        queries, key_new, value_new = split_heads(projected, lengths, KVH, HD)
        entries.append(jnp.stack([key_new.reshape(REQUESTS, KVH * HD), value_new.reshape(REQUESTS, KVH * HD)]))
        grouped = (queries.reshape(blocks, REQ_DEV, KVH, GROUP, HD), key_new.reshape(blocks, REQ_DEV, KVH, HD), value_new.reshape(blocks, REQ_DEV, KVH, HD), kv_cache[layer_index, 0].reshape(blocks, CACHE_TOK, KVH * HD), kv_cache[layer_index, 1].reshape(blocks, CACHE_TOK, KVH * HD), lengths.reshape(blocks, REQ_DEV))
        attended = lax.map(attend_item, grouped).reshape(REQUESTS, HQ * HD)
        summed = jnp.dot(attended, o_weight, preferred_element_type=jnp.float32)
        stream = (stream.astype(jnp.float32) + summed).astype(jnp.bfloat16)
        normed = rms_norm(stream, mlp_gain)
        both_parts = jnp.dot(normed, gate_up.reshape(D, 2 * FF), preferred_element_type=jnp.float32)
        activated = (jax.nn.silu(both_parts[:, :FF]) * both_parts[:, FF:]).astype(jnp.bfloat16)
        summed = jnp.dot(activated, down_weight, preferred_element_type=jnp.float32)
        stream = (stream.astype(jnp.float32) + summed).astype(jnp.bfloat16)
    return (stream, jnp.stack(entries))
```

```python
import math

import jax
import jax.numpy as jnp
from jax import lax
from jax.sharding import PartitionSpec as P

D = 8192
HD = 128
LAYERS = 2


EPSILON = 1e-05
ROPE_BASE = 500000.0


def copy_for_each(shard, axis):
    length = lax.axis_size(axis)
    return lax.all_to_all(
        jnp.broadcast_to(shard[None], (length, *shard.shape)), axis, 0, 0, tiled=True
    )


def of_everyone(shard, axis):
    return copy_for_each(shard, axis).sum(axis=0)


def laid_out(parts, dim):
    parts = jnp.moveaxis(parts, 0, dim)
    lengths = parts.shape
    return parts.reshape(*lengths[:dim], lengths[dim] * lengths[dim + 1], *lengths[dim + 2 :])


def gathered_copies(shard, axis, dim):
    parts = copy_for_each(shard, axis)
    return laid_out(parts, dim)


def in_blocks(shard, dim, length):
    before, after = (shard.shape[:dim], shard.shape[dim + 1 :])
    return jnp.moveaxis(shard.reshape(*before, length, -1, *after), dim, 0)


def summed_on_arrival(shard, axis, dim):
    parts = in_blocks(shard, dim, lax.axis_size(axis))
    arrived = lax.all_to_all(parts, axis, split_axis=0, concat_axis=0, tiled=True)
    return arrived.sum(axis=0)


def sent_and_summed(shard, axis, dim):
    length = lax.axis_size(axis)
    parts = lax.all_to_all(in_blocks(shard, dim, length), axis, 0, 0, tiled=True)
    return jnp.sum(parts.astype(jnp.float32), axis=0)


def scale_rows(floats, square_sum, gain):
    scaled = (
        floats * lax.rsqrt(square_sum / D + EPSILON)[:, None] * gain.astype(jnp.float32)[None, :]
    )
    return scaled.astype(jnp.bfloat16)


def norm_rows(stream, gain):
    floats = stream.astype(jnp.float32)
    square_sum = lax.psum(jnp.sum(floats * floats, axis=1), "wide")
    return lax.all_gather(scale_rows(floats, square_sum, gain), "narrow", axis=0, tiled=True)


def rotate_pairs(vectors, cosine, sine_table):
    half_dim = vectors.shape[-1] // 2
    first_half = vectors[..., :half_dim]
    second_half = vectors[..., half_dim:]
    return jnp.concatenate(
        [
            first_half * cosine - second_half * sine_table,
            second_half * cosine + first_half * sine_table,
        ],
        axis=-1,
    )


def rotary_tables(lengths, head_dim):
    half_dim = head_dim // 2
    inverse = jnp.exp(
        jnp.arange(half_dim, dtype=jnp.float32) * (-2.0 * math.log(ROPE_BASE) / head_dim)
    )
    angles = lengths.astype(jnp.float32)[:, None] * inverse[None, :]
    return (jnp.cos(angles), jnp.sin(angles))


def split_heads(projected, lengths, heads_kv, head_dim):
    row_count = projected.shape[0]
    grouped = projected.reshape(row_count, heads_kv, -1, head_dim)
    group_size = grouped.shape[2] - 2
    cosine, sine_table = rotary_tables(lengths, head_dim)
    rotated = rotate_pairs(
        grouped[:, :, : group_size + 1], cosine[:, None, None, :], sine_table[:, None, None, :]
    )
    queries = rotated[:, :, :group_size].astype(jnp.bfloat16)
    key_new = rotated[:, :, group_size].astype(jnp.bfloat16)
    value_new = grouped[:, :, group_size + 1].astype(jnp.bfloat16)
    return (queries, key_new, value_new)


def attend(queries, key_new, value_new, cached_keys, cached_values, lengths):
    row_count, heads_kv, group_size, head_dim = queries.shape
    slot_count = cached_keys.shape[0]
    score_scale = 1.0 / math.sqrt(head_dim)
    key_table = cached_keys.reshape(slot_count, heads_kv, head_dim)
    value_table = cached_values.reshape(slot_count, heads_kv, head_dim)
    starts = jnp.cumsum(lengths) - lengths
    position = jnp.arange(slot_count, dtype=jnp.int32)
    owned = (position[None, :] >= starts[:, None]) & (
        position[None, :] < (starts + lengths)[:, None]
    )
    scores = (
        jnp.einsum("rkgd,tkd->krgt", queries, key_table, preferred_element_type=jnp.float32)
        * score_scale
    )
    scores = jnp.where(owned[None, :, None, :], scores, -jnp.inf)
    own_score = (
        jnp.einsum("rkgd,rkd->krg", queries, key_new, preferred_element_type=jnp.float32)
        * score_scale
    )
    row_peak = jnp.maximum(jnp.max(scores, axis=3), own_score)
    weights = jnp.exp(scores - row_peak[..., None])
    own_weight = jnp.exp(own_score - row_peak)
    weight_sum = jnp.sum(weights, axis=3) + own_weight
    blended = jnp.einsum(
        "krgt,tkd->krgd",
        weights.astype(jnp.bfloat16),
        value_table,
        preferred_element_type=jnp.float32,
    )
    own_rounded = lax.optimization_barrier(own_weight.astype(jnp.bfloat16)).astype(jnp.float32)
    blended = blended + own_rounded[..., None] * jnp.transpose(value_new, (1, 0, 2))[
        :, :, None, :
    ].astype(jnp.float32)
    normalized = (blended / weight_sum[..., None]).astype(jnp.bfloat16)
    return jnp.transpose(normalized, (1, 0, 2, 3)).reshape(
        row_count, heads_kv * group_size * head_dim
    )


def on_device(
    hidden_in, lengths, kv_cache, qkv_weight, o_weight, gate_up, down_weight, attn_gain, mlp_gain
):
    width_dev = hidden_in.shape[1]
    heads_kv = qkv_weight.shape[1]
    flat_qkv = qkv_weight.reshape(width_dev, -1)
    stream = hidden_in
    entries = []
    for layer_index in range(LAYERS):
        normed = norm_rows(stream, attn_gain)
        own_qkv = lax.psum_scatter(
            jnp.dot(normed, flat_qkv, preferred_element_type=jnp.float32),
            "wide",
            scatter_dimension=0,
            tiled=True,
        )
        queries, key_new, value_new = split_heads(own_qkv, lengths, heads_kv, HD)
        own_rows = key_new.shape[0]
        entries.append(
            jnp.stack(
                [
                    key_new.reshape(own_rows, heads_kv * HD),
                    value_new.reshape(own_rows, heads_kv * HD),
                ]
            )
        )
        attended = attend(
            queries, key_new, value_new, kv_cache[layer_index, 0], kv_cache[layer_index, 1], lengths
        )
        heads_all = lax.all_gather(attended, "wide", axis=0, tiled=True)
        summed = lax.psum_scatter(
            jnp.dot(heads_all, o_weight, preferred_element_type=jnp.float32),
            "narrow",
            scatter_dimension=0,
            tiled=True,
        )
        stream = (stream.astype(jnp.float32) + summed).astype(jnp.bfloat16)
        normed = norm_rows(stream, mlp_gain)
        both_parts = jnp.einsum(
            "rd,dkh->rkh", normed, gate_up, preferred_element_type=jnp.float32
        )
        own_rows_parts = lax.psum_scatter(
            both_parts.astype(jnp.bfloat16), "wide", scatter_dimension=0, tiled=True
        ).astype(jnp.float32)
        activated = (jax.nn.silu(own_rows_parts[:, 0]) * own_rows_parts[:, 1]).astype(jnp.bfloat16)
        partial_down = jnp.dot(
            lax.all_gather(activated, "wide", axis=0, tiled=True),
            down_weight,
            preferred_element_type=jnp.float32,
        )
        summed = lax.psum_scatter(partial_down, "narrow", scatter_dimension=0, tiled=True)
        stream = (stream.astype(jnp.float32) + summed).astype(jnp.bfloat16)
    return (stream, jnp.stack(entries))


def solution(mesh):
    return jax.shard_map(
        on_device,
        mesh=mesh,
        in_specs=(
            P("narrow", "wide"),
            P("wide"),
            P(None, None, "wide", "narrow"),
            P("wide", "narrow", None),
            P("narrow", "wide"),
            P("wide", None, "narrow"),
            P("narrow", "wide"),
            P("wide"),
            P("wide"),
        ),
        out_specs=(P("narrow", "wide"), P(None, None, "wide", "narrow")),
        check_vma=False,
    )
```

```python
import math

import jax
import jax.numpy as jnp
from jax import lax
from jax.sharding import PartitionSpec as P

D = 8192
HD = 128
LAYERS = 2


EPSILON = 1e-05
ROPE_BASE = 500000.0


def copy_for_each(shard, axis):
    length = lax.axis_size(axis)
    return lax.all_to_all(
        jnp.broadcast_to(shard[None], (length, *shard.shape)), axis, 0, 0, tiled=True
    )


def of_everyone(shard, axis):
    return copy_for_each(shard, axis).sum(axis=0)


def laid_out(parts, dim):
    parts = jnp.moveaxis(parts, 0, dim)
    lengths = parts.shape
    return parts.reshape(*lengths[:dim], lengths[dim] * lengths[dim + 1], *lengths[dim + 2 :])


def gathered_copies(shard, axis, dim):
    parts = copy_for_each(shard, axis)
    return laid_out(parts, dim)


def in_blocks(shard, dim, length):
    before, after = (shard.shape[:dim], shard.shape[dim + 1 :])
    return jnp.moveaxis(shard.reshape(*before, length, -1, *after), dim, 0)


def summed_on_arrival(shard, axis, dim):
    parts = in_blocks(shard, dim, lax.axis_size(axis))
    arrived = lax.all_to_all(parts, axis, split_axis=0, concat_axis=0, tiled=True)
    return arrived.sum(axis=0)


def sent_and_summed(shard, axis, dim):
    length = lax.axis_size(axis)
    parts = lax.all_to_all(in_blocks(shard, dim, length), axis, 0, 0, tiled=True)
    return jnp.sum(parts.astype(jnp.float32), axis=0)


def scale_rows(floats, square_sum, gain):
    scaled = (
        floats * lax.rsqrt(square_sum / D + EPSILON)[:, None] * gain.astype(jnp.float32)[None, :]
    )
    return scaled.astype(jnp.bfloat16)


def norm_rows(stream, gain):
    floats = stream.astype(jnp.float32)
    square_sum = of_everyone(jnp.sum(floats * floats, axis=1), "wide")
    return gathered_copies(scale_rows(floats, square_sum, gain), "narrow", 0)


def rotate_pairs(vectors, cosine, sine_table):
    half_dim = vectors.shape[-1] // 2
    first_half = vectors[..., :half_dim]
    second_half = vectors[..., half_dim:]
    return jnp.concatenate(
        [
            first_half * cosine - second_half * sine_table,
            second_half * cosine + first_half * sine_table,
        ],
        axis=-1,
    )


def rotary_tables(lengths, head_dim):
    half_dim = head_dim // 2
    inverse = jnp.exp(
        jnp.arange(half_dim, dtype=jnp.float32) * (-2.0 * math.log(ROPE_BASE) / head_dim)
    )
    angles = lengths.astype(jnp.float32)[:, None] * inverse[None, :]
    return (jnp.cos(angles), jnp.sin(angles))


def split_heads(projected, lengths, heads_kv, head_dim):
    row_count = projected.shape[0]
    grouped = projected.reshape(row_count, heads_kv, -1, head_dim)
    group_size = grouped.shape[2] - 2
    cosine, sine_table = rotary_tables(lengths, head_dim)
    rotated = rotate_pairs(
        grouped[:, :, : group_size + 1], cosine[:, None, None, :], sine_table[:, None, None, :]
    )
    queries = rotated[:, :, :group_size].astype(jnp.bfloat16)
    key_new = rotated[:, :, group_size].astype(jnp.bfloat16)
    value_new = grouped[:, :, group_size + 1].astype(jnp.bfloat16)
    return (queries, key_new, value_new)


def attend(queries, key_new, value_new, cached_keys, cached_values, lengths):
    row_count, heads_kv, group_size, head_dim = queries.shape
    slot_count = cached_keys.shape[0]
    score_scale = 1.0 / math.sqrt(head_dim)
    key_table = cached_keys.reshape(slot_count, heads_kv, head_dim)
    value_table = cached_values.reshape(slot_count, heads_kv, head_dim)
    starts = jnp.cumsum(lengths) - lengths
    position = jnp.arange(slot_count, dtype=jnp.int32)
    owned = (position[None, :] >= starts[:, None]) & (
        position[None, :] < (starts + lengths)[:, None]
    )
    scores = (
        jnp.einsum("rkgd,tkd->krgt", queries, key_table, preferred_element_type=jnp.float32)
        * score_scale
    )
    scores = jnp.where(owned[None, :, None, :], scores, -jnp.inf)
    own_score = (
        jnp.einsum("rkgd,rkd->krg", queries, key_new, preferred_element_type=jnp.float32)
        * score_scale
    )
    row_peak = jnp.maximum(jnp.max(scores, axis=3), own_score)
    weights = jnp.exp(scores - row_peak[..., None])
    own_weight = jnp.exp(own_score - row_peak)
    weight_sum = jnp.sum(weights, axis=3) + own_weight
    blended = jnp.einsum(
        "krgt,tkd->krgd",
        weights.astype(jnp.bfloat16),
        value_table,
        preferred_element_type=jnp.float32,
    )
    own_rounded = lax.optimization_barrier(own_weight.astype(jnp.bfloat16)).astype(jnp.float32)
    blended = blended + own_rounded[..., None] * jnp.transpose(value_new, (1, 0, 2))[
        :, :, None, :
    ].astype(jnp.float32)
    normalized = (blended / weight_sum[..., None]).astype(jnp.bfloat16)
    return jnp.transpose(normalized, (1, 0, 2, 3)).reshape(
        row_count, heads_kv * group_size * head_dim
    )


def split_hi_lo(values):
    high = values.astype(jnp.bfloat16)
    low = (values - high.astype(jnp.float32)).astype(jnp.bfloat16)
    return high, low


def gathered_rows(stream, gain):
    floats = stream.astype(jnp.float32)
    square_sum = jnp.sum(floats * floats, axis=1)
    scaled = (floats * gain.astype(jnp.float32)[None, :]).astype(jnp.bfloat16)
    high, low = split_hi_lo(square_sum)
    packed = jnp.concatenate([scaled, high[:, None], low[:, None]], axis=1)
    rows = gathered_copies(packed, "narrow", 0)
    width = stream.shape[1]
    partial_sum = rows[:, width].astype(jnp.float32) + rows[:, width + 1].astype(jnp.float32)
    return rows[:, :width], partial_sum


def row_scale(square_sum):
    return lax.rsqrt(square_sum / D + EPSILON)


def on_device(
    hidden_in, lengths, kv_cache, qkv_weight, o_weight, gate_up, down_weight, attn_gain, mlp_gain
):
    width_dev = hidden_in.shape[1]
    heads_kv = qkv_weight.shape[1]
    hidden_dev = down_weight.shape[0]
    flat_qkv = qkv_weight.reshape(width_dev, -1)
    stream = hidden_in
    entries = []
    for layer_index in range(LAYERS):
        rows_in = norm_rows(stream, attn_gain)
        own_qkv = summed_on_arrival(
            jnp.dot(rows_in, flat_qkv, preferred_element_type=jnp.float32), "wide", 0
        )
        queries, key_new, value_new = split_heads(own_qkv, lengths, heads_kv, HD)
        own_rows = key_new.shape[0]
        entries.append(
            jnp.stack(
                [
                    key_new.reshape(own_rows, heads_kv * HD),
                    value_new.reshape(own_rows, heads_kv * HD),
                ]
            )
        )
        attended = attend(
            queries, key_new, value_new, kv_cache[layer_index, 0], kv_cache[layer_index, 1], lengths
        )
        heads_all = gathered_copies(attended, "wide", 0)
        summed = summed_on_arrival(
            jnp.dot(heads_all, o_weight, preferred_element_type=jnp.float32), "narrow", 0
        )
        stream = (stream.astype(jnp.float32) + summed).astype(jnp.bfloat16)
        rows_in, partial_sum = gathered_rows(stream, mlp_gain)
        gate_part = jnp.dot(rows_in, gate_up[:, 0, :], preferred_element_type=jnp.float32)
        up_part = jnp.dot(rows_in, gate_up[:, 1, :], preferred_element_type=jnp.float32)
        high, low = split_hi_lo(partial_sum)
        own = sent_and_summed(
            jnp.concatenate(
                [
                    gate_part.astype(jnp.bfloat16),
                    up_part.astype(jnp.bfloat16),
                    high[:, None],
                    low[:, None],
                ],
                axis=1,
            ),
            "wide",
            0,
        )
        scale = row_scale(own[:, 2 * hidden_dev] + own[:, 2 * hidden_dev + 1])[:, None]
        gate = own[:, :hidden_dev] * scale
        up = own[:, hidden_dev : 2 * hidden_dev] * scale
        activated = (jax.nn.silu(gate) * up).astype(jnp.bfloat16)
        partial_down = jnp.dot(
            gathered_copies(activated, "wide", 0), down_weight, preferred_element_type=jnp.float32
        )
        summed = summed_on_arrival(partial_down, "narrow", 0)
        stream = (stream.astype(jnp.float32) + summed).astype(jnp.bfloat16)
    return (stream, jnp.stack(entries))


def solution(mesh):
    return jax.shard_map(
        on_device,
        mesh=mesh,
        in_specs=(
            P("narrow", "wide"),
            P("wide"),
            P(None, None, "wide", "narrow"),
            P("wide", "narrow", None),
            P("narrow", "wide"),
            P("wide", None, "narrow"),
            P("narrow", "wide"),
            P("wide"),
            P("wide"),
        ),
        out_specs=(P("narrow", "wide"), P(None, None, "wide", "narrow")),
        check_vma=False,
    )
```

```python
import math

import jax
import jax.numpy as jnp
from jax import lax
from jax.sharding import PartitionSpec as P

D = 8192
HD = 128
LAYERS = 2


EPSILON = 1e-05
ROPE_BASE = 500000.0


def copy_for_each(shard, axis):
    length = lax.axis_size(axis)
    return lax.all_to_all(
        jnp.broadcast_to(shard[None], (length, *shard.shape)), axis, 0, 0, tiled=True
    )


def of_everyone(shard, axis):
    return copy_for_each(shard, axis).sum(axis=0)


def laid_out(parts, dim):
    parts = jnp.moveaxis(parts, 0, dim)
    lengths = parts.shape
    return parts.reshape(*lengths[:dim], lengths[dim] * lengths[dim + 1], *lengths[dim + 2 :])


def gathered_copies(shard, axis, dim):
    parts = copy_for_each(shard, axis)
    return laid_out(parts, dim)


def in_blocks(shard, dim, length):
    before, after = (shard.shape[:dim], shard.shape[dim + 1 :])
    return jnp.moveaxis(shard.reshape(*before, length, -1, *after), dim, 0)


def summed_on_arrival(shard, axis, dim):
    parts = in_blocks(shard, dim, lax.axis_size(axis))
    arrived = lax.all_to_all(parts, axis, split_axis=0, concat_axis=0, tiled=True)
    return arrived.sum(axis=0)


def sent_and_summed(shard, axis, dim):
    length = lax.axis_size(axis)
    parts = lax.all_to_all(in_blocks(shard, dim, length), axis, 0, 0, tiled=True)
    return jnp.sum(parts.astype(jnp.float32), axis=0)


def scale_rows(floats, square_sum, gain):
    scaled = (
        floats * lax.rsqrt(square_sum / D + EPSILON)[:, None] * gain.astype(jnp.float32)[None, :]
    )
    return scaled.astype(jnp.bfloat16)


def norm_rows(stream, gain):
    floats = stream.astype(jnp.float32)
    square_sum = of_everyone(jnp.sum(floats * floats, axis=1), "wide")
    return gathered_copies(scale_rows(floats, square_sum, gain), "narrow", 0)


def rotate_pairs(vectors, cosine, sine_table):
    half_dim = vectors.shape[-1] // 2
    first_half = vectors[..., :half_dim]
    second_half = vectors[..., half_dim:]
    return jnp.concatenate(
        [
            first_half * cosine - second_half * sine_table,
            second_half * cosine + first_half * sine_table,
        ],
        axis=-1,
    )


def rotary_tables(lengths, head_dim):
    half_dim = head_dim // 2
    inverse = jnp.exp(
        jnp.arange(half_dim, dtype=jnp.float32) * (-2.0 * math.log(ROPE_BASE) / head_dim)
    )
    angles = lengths.astype(jnp.float32)[:, None] * inverse[None, :]
    return (jnp.cos(angles), jnp.sin(angles))


def split_heads(projected, lengths, heads_kv, head_dim):
    row_count = projected.shape[0]
    grouped = projected.reshape(row_count, heads_kv, -1, head_dim)
    group_size = grouped.shape[2] - 2
    cosine, sine_table = rotary_tables(lengths, head_dim)
    rotated = rotate_pairs(
        grouped[:, :, : group_size + 1], cosine[:, None, None, :], sine_table[:, None, None, :]
    )
    queries = rotated[:, :, :group_size].astype(jnp.bfloat16)
    key_new = rotated[:, :, group_size].astype(jnp.bfloat16)
    value_new = grouped[:, :, group_size + 1].astype(jnp.bfloat16)
    return (queries, key_new, value_new)


def attend(queries, key_new, value_new, cached_keys, cached_values, lengths):
    row_count, heads_kv, group_size, head_dim = queries.shape
    slot_count = cached_keys.shape[0]
    score_scale = 1.0 / math.sqrt(head_dim)
    key_table = cached_keys.reshape(slot_count, heads_kv, head_dim)
    value_table = cached_values.reshape(slot_count, heads_kv, head_dim)
    starts = jnp.cumsum(lengths) - lengths
    position = jnp.arange(slot_count, dtype=jnp.int32)
    owned = (position[None, :] >= starts[:, None]) & (
        position[None, :] < (starts + lengths)[:, None]
    )
    scores = (
        jnp.einsum("rkgd,tkd->krgt", queries, key_table, preferred_element_type=jnp.float32)
        * score_scale
    )
    scores = jnp.where(owned[None, :, None, :], scores, -jnp.inf)
    own_score = (
        jnp.einsum("rkgd,rkd->krg", queries, key_new, preferred_element_type=jnp.float32)
        * score_scale
    )
    row_peak = jnp.maximum(jnp.max(scores, axis=3), own_score)
    weights = jnp.exp(scores - row_peak[..., None])
    own_weight = jnp.exp(own_score - row_peak)
    weight_sum = jnp.sum(weights, axis=3) + own_weight
    blended = jnp.einsum(
        "krgt,tkd->krgd",
        weights.astype(jnp.bfloat16),
        value_table,
        preferred_element_type=jnp.float32,
    )
    own_rounded = lax.optimization_barrier(own_weight.astype(jnp.bfloat16)).astype(jnp.float32)
    blended = blended + own_rounded[..., None] * jnp.transpose(value_new, (1, 0, 2))[
        :, :, None, :
    ].astype(jnp.float32)
    normalized = (blended / weight_sum[..., None]).astype(jnp.bfloat16)
    return jnp.transpose(normalized, (1, 0, 2, 3)).reshape(
        row_count, heads_kv * group_size * head_dim
    )


def split_hi_lo(values):
    high = values.astype(jnp.bfloat16)
    low = (values - high.astype(jnp.float32)).astype(jnp.bfloat16)
    return high, low


def gathered_rows(stream, gain):
    floats = stream.astype(jnp.float32)
    square_sum = jnp.sum(floats * floats, axis=1)
    scaled = (floats * gain.astype(jnp.float32)[None, :]).astype(jnp.bfloat16)
    high, low = split_hi_lo(square_sum)
    packed = jnp.concatenate([scaled, high[:, None], low[:, None]], axis=1)
    rows = gathered_copies(packed, "narrow", 0)
    width = stream.shape[1]
    partial_sum = rows[:, width].astype(jnp.float32) + rows[:, width + 1].astype(jnp.float32)
    return rows[:, :width], partial_sum


def row_scale(square_sum):
    return lax.rsqrt(square_sum / D + EPSILON)


def on_device(
    hidden_in, lengths, kv_cache, qkv_weight, o_weight, gate_up, down_weight, attn_gain, mlp_gain
):
    width_dev = hidden_in.shape[1]
    heads_kv = qkv_weight.shape[1]
    hidden_dev = down_weight.shape[0]
    flat_qkv = qkv_weight.reshape(width_dev, -1)
    stream = hidden_in
    entries = []
    for layer_index in range(LAYERS):
        rows_in = norm_rows(stream, attn_gain)
        own_qkv = summed_on_arrival(
            jnp.dot(rows_in, flat_qkv, preferred_element_type=jnp.float32), "wide", 0
        )
        queries, key_new, value_new = split_heads(own_qkv, lengths, heads_kv, HD)
        own_rows = key_new.shape[0]
        entries.append(
            jnp.stack(
                [
                    key_new.reshape(own_rows, heads_kv * HD),
                    value_new.reshape(own_rows, heads_kv * HD),
                ]
            )
        )
        attended = attend(
            queries, key_new, value_new, kv_cache[layer_index, 0], kv_cache[layer_index, 1], lengths
        )
        heads_all = gathered_copies(attended, "wide", 0)
        summed = summed_on_arrival(
            jnp.dot(heads_all, o_weight, preferred_element_type=jnp.float32), "narrow", 0
        )
        stream = (stream.astype(jnp.float32) + summed).astype(jnp.bfloat16)
        rows_in, partial_sum = gathered_rows(stream, mlp_gain)
        both_parts = jnp.einsum(
            "rd,dkh->krh", rows_in, gate_up, preferred_element_type=jnp.float32
        ).astype(jnp.bfloat16)
        high, low = split_hi_lo(partial_sum)
        sums_col = jnp.stack([high, low])[:, :, None]
        payload = jnp.concatenate([both_parts, sums_col], axis=2)
        wide_size = lax.axis_size("wide")
        payload = payload.reshape(2, wide_size, -1, hidden_dev + 1)
        arrived = lax.all_to_all(payload, "wide", 1, 1, tiled=True)
        own = jnp.sum(arrived.astype(jnp.float32), axis=1)
        scale = row_scale(own[0, :, hidden_dev] + own[1, :, hidden_dev])[:, None]
        gate = own[0, :, :hidden_dev] * scale
        up = own[1, :, :hidden_dev] * scale
        activated = (jax.nn.silu(gate) * up).astype(jnp.bfloat16)
        partial_down = jnp.dot(
            gathered_copies(activated, "wide", 0), down_weight, preferred_element_type=jnp.float32
        )
        summed = summed_on_arrival(partial_down, "narrow", 0)
        stream = (stream.astype(jnp.float32) + summed).astype(jnp.bfloat16)
    return (stream, jnp.stack(entries))


def solution(mesh):
    return jax.shard_map(
        on_device,
        mesh=mesh,
        in_specs=(
            P("narrow", "wide"),
            P("wide"),
            P(None, None, "wide", "narrow"),
            P("wide", "narrow", None),
            P("narrow", "wide"),
            P("wide", None, "narrow"),
            P("narrow", "wide"),
            P("wide"),
            P("wide"),
        ),
        out_specs=(P("narrow", "wide"), P(None, None, "wide", "narrow")),
        check_vma=False,
    )
```

```python
import math

import jax
import jax.numpy as jnp
from jax import lax
from jax.sharding import PartitionSpec as P

D = 8192
HD = 128
LAYERS = 2


EPSILON = 1e-05
ROPE_BASE = 500000.0


def copy_for_each(shard, axis):
    length = lax.axis_size(axis)
    return lax.all_to_all(
        jnp.broadcast_to(shard[None], (length, *shard.shape)), axis, 0, 0, tiled=True
    )


def of_everyone(shard, axis):
    return copy_for_each(shard, axis).sum(axis=0)


def laid_out(parts, dim):
    parts = jnp.moveaxis(parts, 0, dim)
    lengths = parts.shape
    return parts.reshape(*lengths[:dim], lengths[dim] * lengths[dim + 1], *lengths[dim + 2 :])


def gathered_copies(shard, axis, dim):
    parts = copy_for_each(shard, axis)
    return laid_out(parts, dim)


def in_blocks(shard, dim, length):
    before, after = (shard.shape[:dim], shard.shape[dim + 1 :])
    return jnp.moveaxis(shard.reshape(*before, length, -1, *after), dim, 0)


def summed_on_arrival(shard, axis, dim):
    parts = in_blocks(shard, dim, lax.axis_size(axis))
    arrived = lax.all_to_all(parts, axis, split_axis=0, concat_axis=0, tiled=True)
    return arrived.sum(axis=0)


def sent_and_summed(shard, axis, dim):
    length = lax.axis_size(axis)
    parts = lax.all_to_all(in_blocks(shard, dim, length), axis, 0, 0, tiled=True)
    return jnp.sum(parts.astype(jnp.float32), axis=0)


def scale_rows(floats, square_sum, gain):
    scaled = (
        floats * lax.rsqrt(square_sum / D + EPSILON)[:, None] * gain.astype(jnp.float32)[None, :]
    )
    return scaled.astype(jnp.bfloat16)


def norm_rows(stream, gain):
    floats = stream.astype(jnp.float32)
    square_sum = of_everyone(jnp.sum(floats * floats, axis=1), "wide")
    return gathered_copies(scale_rows(floats, square_sum, gain), "narrow", 0)


def rotate_pairs(vectors, cosine, sine_table):
    half_dim = vectors.shape[-1] // 2
    first_half = vectors[..., :half_dim]
    second_half = vectors[..., half_dim:]
    return jnp.concatenate(
        [
            first_half * cosine - second_half * sine_table,
            second_half * cosine + first_half * sine_table,
        ],
        axis=-1,
    )


def rotary_tables(lengths, head_dim):
    half_dim = head_dim // 2
    inverse = jnp.exp(
        jnp.arange(half_dim, dtype=jnp.float32) * (-2.0 * math.log(ROPE_BASE) / head_dim)
    )
    angles = lengths.astype(jnp.float32)[:, None] * inverse[None, :]
    return (jnp.cos(angles), jnp.sin(angles))


def split_heads(projected, lengths, heads_kv, head_dim):
    row_count = projected.shape[0]
    grouped = projected.reshape(row_count, heads_kv, -1, head_dim)
    group_size = grouped.shape[2] - 2
    cosine, sine_table = rotary_tables(lengths, head_dim)
    rotated = rotate_pairs(
        grouped[:, :, : group_size + 1], cosine[:, None, None, :], sine_table[:, None, None, :]
    )
    queries = rotated[:, :, :group_size].astype(jnp.bfloat16)
    key_new = rotated[:, :, group_size].astype(jnp.bfloat16)
    value_new = grouped[:, :, group_size + 1].astype(jnp.bfloat16)
    return (queries, key_new, value_new)


def attend(queries, key_new, value_new, cached_keys, cached_values, lengths):
    row_count, heads_kv, group_size, head_dim = queries.shape
    slot_count = cached_keys.shape[0]
    score_scale = 1.0 / math.sqrt(head_dim)
    key_table = cached_keys.reshape(slot_count, heads_kv, head_dim)
    value_table = cached_values.reshape(slot_count, heads_kv, head_dim)
    starts = jnp.cumsum(lengths) - lengths
    position = jnp.arange(slot_count, dtype=jnp.int32)
    owned = (position[None, :] >= starts[:, None]) & (
        position[None, :] < (starts + lengths)[:, None]
    )
    scores = (
        jnp.einsum("rkgd,tkd->krgt", queries, key_table, preferred_element_type=jnp.float32)
        * score_scale
    )
    scores = jnp.where(owned[None, :, None, :], scores, -jnp.inf)
    own_score = (
        jnp.einsum("rkgd,rkd->krg", queries, key_new, preferred_element_type=jnp.float32)
        * score_scale
    )
    row_peak = jnp.maximum(jnp.max(scores, axis=3), own_score)
    weights = jnp.exp(scores - row_peak[..., None])
    own_weight = jnp.exp(own_score - row_peak)
    weight_sum = jnp.sum(weights, axis=3) + own_weight
    blended = jnp.einsum(
        "krgt,tkd->krgd",
        weights.astype(jnp.bfloat16),
        value_table,
        preferred_element_type=jnp.float32,
    )
    own_rounded = lax.optimization_barrier(own_weight.astype(jnp.bfloat16)).astype(jnp.float32)
    blended = blended + own_rounded[..., None] * jnp.transpose(value_new, (1, 0, 2))[
        :, :, None, :
    ].astype(jnp.float32)
    normalized = (blended / weight_sum[..., None]).astype(jnp.bfloat16)
    return jnp.transpose(normalized, (1, 0, 2, 3)).reshape(
        row_count, heads_kv * group_size * head_dim
    )


def split_hi_lo(values):
    high = values.astype(jnp.bfloat16)
    low = (values - high.astype(jnp.float32)).astype(jnp.bfloat16)
    return high, low


def gathered_rows(stream, gain):
    floats = stream.astype(jnp.float32)
    square_sum = jnp.sum(floats * floats, axis=1)
    scaled = (floats * gain.astype(jnp.float32)[None, :]).astype(jnp.bfloat16)
    high, low = split_hi_lo(square_sum)
    packed = jnp.concatenate([scaled, high[:, None], low[:, None]], axis=1)
    rows = gathered_copies(packed, "narrow", 0)
    width = stream.shape[1]
    partial_sum = rows[:, width].astype(jnp.float32) + rows[:, width + 1].astype(jnp.float32)
    return rows[:, :width], partial_sum


def row_scale(square_sum):
    return lax.rsqrt(square_sum / D + EPSILON)


def on_device(
    hidden_in, lengths, kv_cache, qkv_weight, o_weight, gate_up, down_weight, attn_gain, mlp_gain
):
    width_dev = hidden_in.shape[1]
    heads_kv = qkv_weight.shape[1]
    hidden_dev = down_weight.shape[0]
    flat_qkv = qkv_weight.reshape(width_dev, -1)
    stream = hidden_in
    entries = []
    for layer_index in range(LAYERS):
        if layer_index == 0:
            rows_in = norm_rows(stream, attn_gain)
            own_qkv = summed_on_arrival(
                jnp.dot(rows_in, flat_qkv, preferred_element_type=jnp.float32), "wide", 0
            )
        else:
            rows_in, partial_sum = gathered_rows(stream, attn_gain)
            projected = jnp.dot(rows_in, flat_qkv, preferred_element_type=jnp.float32)
            own = summed_on_arrival(
                jnp.concatenate([projected, partial_sum[:, None]], axis=1), "wide", 0
            )
            qkv_cols = flat_qkv.shape[1]
            own_qkv = own[:, :qkv_cols] * row_scale(own[:, qkv_cols])[:, None]
        queries, key_new, value_new = split_heads(own_qkv, lengths, heads_kv, HD)
        own_rows = key_new.shape[0]
        entries.append(
            jnp.stack(
                [
                    key_new.reshape(own_rows, heads_kv * HD),
                    value_new.reshape(own_rows, heads_kv * HD),
                ]
            )
        )
        attended = attend(
            queries, key_new, value_new, kv_cache[layer_index, 0], kv_cache[layer_index, 1], lengths
        )
        heads_all = gathered_copies(attended, "wide", 0)
        summed = summed_on_arrival(
            jnp.dot(heads_all, o_weight, preferred_element_type=jnp.float32), "narrow", 0
        )
        stream = (stream.astype(jnp.float32) + summed).astype(jnp.bfloat16)
        rows_in, partial_sum = gathered_rows(stream, mlp_gain)
        both_parts = jnp.einsum(
            "rd,dkh->krh", rows_in, gate_up, preferred_element_type=jnp.float32
        ).astype(jnp.bfloat16)
        high, low = split_hi_lo(partial_sum)
        sums_col = jnp.stack([high, low])[:, :, None]
        payload = jnp.concatenate([both_parts, sums_col], axis=2)
        wide_size = lax.axis_size("wide")
        payload = payload.reshape(2, wide_size, -1, hidden_dev + 1)
        arrived = lax.all_to_all(payload, "wide", 1, 1, tiled=True)
        own = jnp.sum(arrived.astype(jnp.float32), axis=1)
        scale = row_scale(own[0, :, hidden_dev] + own[1, :, hidden_dev])[:, None]
        gate = own[0, :, :hidden_dev] * scale
        up = own[1, :, :hidden_dev] * scale
        activated = (jax.nn.silu(gate) * up).astype(jnp.bfloat16)
        partial_down = jnp.dot(
            gathered_copies(activated, "wide", 0), down_weight, preferred_element_type=jnp.float32
        )
        summed = summed_on_arrival(partial_down, "narrow", 0)
        stream = (stream.astype(jnp.float32) + summed).astype(jnp.bfloat16)
    return (stream, jnp.stack(entries))


def solution(mesh):
    return jax.shard_map(
        on_device,
        mesh=mesh,
        in_specs=(
            P("narrow", "wide"),
            P("wide"),
            P(None, None, "wide", "narrow"),
            P("wide", "narrow", None),
            P("narrow", "wide"),
            P("wide", None, "narrow"),
            P("narrow", "wide"),
            P("wide"),
            P("wide"),
        ),
        out_specs=(P("narrow", "wide"), P(None, None, "wide", "narrow")),
        check_vma=False,
    )
```

```python
import math

import jax
import jax.numpy as jnp
from jax import lax
from jax.sharding import Mesh
from jax.sharding import PartitionSpec as P

D = 8192
HD = 128
LAYERS = 2
CHIPS = "chips"
CORES = "cores"
WIDE = (CHIPS, CORES)


EPSILON = 1e-05
ROPE_BASE = 500000.0


def axis_length(axis):
    if isinstance(axis, tuple):
        return math.prod(lax.axis_size(name) for name in axis)
    return lax.axis_size(axis)


def swap_cores(shard):
    return lax.ppermute(shard, CORES, [(0, 1), (1, 0)])


def reduced_rows(partial, row_dim, wire_type):
    chips = lax.axis_size(CHIPS)
    shape = partial.shape
    split = shape[:row_dim] + (chips, 2, shape[row_dim] // (chips * 2)) + shape[row_dim + 1 :]
    blocks = partial.reshape(split)
    core = lax.axis_index(CORES)
    mine = lax.dynamic_index_in_dim(blocks, core, row_dim + 1, keepdims=False)
    other = lax.dynamic_index_in_dim(blocks, 1 - core, row_dim + 1, keepdims=False)
    pair_sum = mine.astype(jnp.float32) + swap_cores(other).astype(jnp.float32)
    return pair_sum, row_dim


def chip_sum(pair_sum, row_dim, wire_type):
    arrived = lax.all_to_all(pair_sum.astype(wire_type), CHIPS, row_dim, row_dim, tiled=True)
    return jnp.sum(arrived.astype(jnp.float32), axis=row_dim)


def gathered_rows_wide(shard):
    chips = lax.axis_size(CHIPS)
    from_chips = lax.all_to_all(
        jnp.broadcast_to(shard[None], (chips, *shard.shape)), CHIPS, 0, 0, tiled=True
    )
    from_partner = swap_cores(from_chips)
    first = lax.axis_index(CORES) == 0
    low_core = jnp.where(first, from_chips, from_partner)
    high_core = jnp.where(first, from_partner, from_chips)
    return jnp.stack([low_core, high_core], axis=1).reshape(-1, *shard.shape[1:])


def copy_for_each(shard, axis):
    length = axis_length(axis)
    return lax.all_to_all(
        jnp.broadcast_to(shard[None], (length, *shard.shape)), axis, 0, 0, tiled=True
    )


def of_everyone(shard, axis):
    return copy_for_each(shard, axis).sum(axis=0)


def laid_out(parts, dim):
    parts = jnp.moveaxis(parts, 0, dim)
    lengths = parts.shape
    return parts.reshape(*lengths[:dim], lengths[dim] * lengths[dim + 1], *lengths[dim + 2 :])


def gathered_copies(shard, axis, dim):
    parts = copy_for_each(shard, axis)
    return laid_out(parts, dim)


def in_blocks(shard, dim, length):
    before, after = (shard.shape[:dim], shard.shape[dim + 1 :])
    return jnp.moveaxis(shard.reshape(*before, length, -1, *after), dim, 0)


def summed_on_arrival(shard, axis, dim):
    parts = in_blocks(shard, dim, axis_length(axis))
    arrived = lax.all_to_all(parts, axis, split_axis=0, concat_axis=0, tiled=True)
    return arrived.sum(axis=0)


def sent_and_summed(shard, axis, dim):
    length = axis_length(axis)
    parts = lax.all_to_all(in_blocks(shard, dim, length), axis, 0, 0, tiled=True)
    return jnp.sum(parts.astype(jnp.float32), axis=0)


def scale_rows(floats, square_sum, gain):
    scaled = (
        floats * lax.rsqrt(square_sum / D + EPSILON)[:, None] * gain.astype(jnp.float32)[None, :]
    )
    return scaled.astype(jnp.bfloat16)


def norm_rows(stream, gain):
    floats = stream.astype(jnp.float32)
    square_sum = of_everyone(jnp.sum(floats * floats, axis=1), WIDE)
    return gathered_copies(scale_rows(floats, square_sum, gain), "narrow", 0)


def rotate_pairs(vectors, cosine, sine_table):
    half_dim = vectors.shape[-1] // 2
    first_half = vectors[..., :half_dim]
    second_half = vectors[..., half_dim:]
    return jnp.concatenate(
        [
            first_half * cosine - second_half * sine_table,
            second_half * cosine + first_half * sine_table,
        ],
        axis=-1,
    )


def rotary_tables(lengths, head_dim):
    half_dim = head_dim // 2
    inverse = jnp.exp(
        jnp.arange(half_dim, dtype=jnp.float32) * (-2.0 * math.log(ROPE_BASE) / head_dim)
    )
    angles = lengths.astype(jnp.float32)[:, None] * inverse[None, :]
    return (jnp.cos(angles), jnp.sin(angles))


def split_heads(projected, lengths, heads_kv, head_dim):
    row_count = projected.shape[0]
    grouped = projected.reshape(row_count, heads_kv, -1, head_dim)
    group_size = grouped.shape[2] - 2
    cosine, sine_table = rotary_tables(lengths, head_dim)
    rotated = rotate_pairs(
        grouped[:, :, : group_size + 1], cosine[:, None, None, :], sine_table[:, None, None, :]
    )
    queries = rotated[:, :, :group_size].astype(jnp.bfloat16)
    key_new = rotated[:, :, group_size].astype(jnp.bfloat16)
    value_new = grouped[:, :, group_size + 1].astype(jnp.bfloat16)
    return (queries, key_new, value_new)


def attend(queries, key_new, value_new, cached_keys, cached_values, lengths):
    row_count, heads_kv, group_size, head_dim = queries.shape
    slot_count = cached_keys.shape[0]
    score_scale = 1.0 / math.sqrt(head_dim)
    key_table = cached_keys.reshape(slot_count, heads_kv, head_dim)
    value_table = cached_values.reshape(slot_count, heads_kv, head_dim)
    starts = jnp.cumsum(lengths) - lengths
    position = jnp.arange(slot_count, dtype=jnp.int32)
    owned = (position[None, :] >= starts[:, None]) & (
        position[None, :] < (starts + lengths)[:, None]
    )
    scores = (
        jnp.einsum("rkgd,tkd->krgt", queries, key_table, preferred_element_type=jnp.float32)
        * score_scale
    )
    scores = jnp.where(owned[None, :, None, :], scores, -jnp.inf)
    own_score = (
        jnp.einsum("rkgd,rkd->krg", queries, key_new, preferred_element_type=jnp.float32)
        * score_scale
    )
    row_peak = jnp.maximum(jnp.max(scores, axis=3), own_score)
    weights = jnp.exp(scores - row_peak[..., None])
    own_weight = jnp.exp(own_score - row_peak)
    weight_sum = jnp.sum(weights, axis=3) + own_weight
    blended = jnp.einsum(
        "krgt,tkd->krgd",
        weights.astype(jnp.bfloat16),
        value_table,
        preferred_element_type=jnp.float32,
    )
    own_rounded = lax.optimization_barrier(own_weight.astype(jnp.bfloat16)).astype(jnp.float32)
    blended = blended + own_rounded[..., None] * jnp.transpose(value_new, (1, 0, 2))[
        :, :, None, :
    ].astype(jnp.float32)
    normalized = (blended / weight_sum[..., None]).astype(jnp.bfloat16)
    return jnp.transpose(normalized, (1, 0, 2, 3)).reshape(
        row_count, heads_kv * group_size * head_dim
    )


def split_hi_lo(values):
    high = values.astype(jnp.bfloat16)
    low = (values - high.astype(jnp.float32)).astype(jnp.bfloat16)
    return high, low


def gathered_rows(stream, gain):
    floats = stream.astype(jnp.float32)
    square_sum = jnp.sum(floats * floats, axis=1)
    scaled = (floats * gain.astype(jnp.float32)[None, :]).astype(jnp.bfloat16)
    high, low = split_hi_lo(square_sum)
    packed = jnp.concatenate([scaled, high[:, None], low[:, None]], axis=1)
    rows = gathered_copies(packed, "narrow", 0)
    width = stream.shape[1]
    partial_sum = rows[:, width].astype(jnp.float32) + rows[:, width + 1].astype(jnp.float32)
    return rows[:, :width], partial_sum


def row_scale(square_sum):
    return lax.rsqrt(square_sum / D + EPSILON)


def on_device(
    hidden_in, lengths, kv_cache, qkv_weight, o_weight, gate_up, down_weight, attn_gain, mlp_gain
):
    width_dev = hidden_in.shape[1]
    heads_kv = qkv_weight.shape[1]
    hidden_dev = down_weight.shape[0]
    flat_qkv = qkv_weight.reshape(width_dev, -1)
    stream = hidden_in
    entries = []
    for layer_index in range(LAYERS):
        if layer_index == 0:
            rows_in = norm_rows(stream, attn_gain)
            pair_sum, row_dim = reduced_rows(
                jnp.dot(rows_in, flat_qkv, preferred_element_type=jnp.float32), 0, jnp.float32
            )
            own_qkv = chip_sum(pair_sum, row_dim, jnp.float32)
        else:
            rows_in, partial_sum = gathered_rows(stream, attn_gain)
            projected = jnp.dot(rows_in, flat_qkv, preferred_element_type=jnp.float32)
            pair_sum, row_dim = reduced_rows(
                jnp.concatenate([projected, partial_sum[:, None]], axis=1), 0, jnp.float32
            )
            own = chip_sum(pair_sum, row_dim, jnp.float32)
            qkv_cols = flat_qkv.shape[1]
            own_qkv = own[:, :qkv_cols] * row_scale(own[:, qkv_cols])[:, None]
        queries, key_new, value_new = split_heads(own_qkv, lengths, heads_kv, HD)
        own_rows = key_new.shape[0]
        entries.append(
            jnp.stack(
                [
                    key_new.reshape(own_rows, heads_kv * HD),
                    value_new.reshape(own_rows, heads_kv * HD),
                ]
            )
        )
        attended = attend(
            queries, key_new, value_new, kv_cache[layer_index, 0], kv_cache[layer_index, 1], lengths
        )
        heads_all = gathered_rows_wide(attended)
        summed = summed_on_arrival(
            jnp.dot(heads_all, o_weight, preferred_element_type=jnp.float32), "narrow", 0
        )
        stream = (stream.astype(jnp.float32) + summed).astype(jnp.bfloat16)
        rows_in, partial_sum = gathered_rows(stream, mlp_gain)
        both_parts = jnp.einsum(
            "rd,dkh->krh", rows_in, gate_up, preferred_element_type=jnp.float32
        ).astype(jnp.bfloat16)
        high, low = split_hi_lo(partial_sum)
        sums_col = jnp.stack([high, low])[:, :, None]
        payload = jnp.concatenate([both_parts, sums_col], axis=2)
        pair_sum, row_dim = reduced_rows(payload, 1, jnp.bfloat16)
        pair_squares = pair_sum[0, :, :, hidden_dev] + pair_sum[1, :, :, hidden_dev]
        high, low = split_hi_lo(pair_squares)
        pair_sum = pair_sum.astype(jnp.bfloat16)
        pair_sum = pair_sum.at[0, :, :, hidden_dev].set(high).at[1, :, :, hidden_dev].set(low)
        own = chip_sum(pair_sum, row_dim, jnp.bfloat16)
        scale = row_scale(own[0, :, hidden_dev] + own[1, :, hidden_dev])[:, None]
        gate = own[0, :, :hidden_dev] * scale
        up = own[1, :, :hidden_dev] * scale
        activated = (jax.nn.silu(gate) * up).astype(jnp.bfloat16)
        partial_down = jnp.dot(
            gathered_rows_wide(activated), down_weight, preferred_element_type=jnp.float32
        )
        summed = summed_on_arrival(partial_down, "narrow", 0)
        stream = (stream.astype(jnp.float32) + summed).astype(jnp.bfloat16)
    return (stream, jnp.stack(entries))


def solution(mesh):
    wide_size, narrow_size = mesh.devices.shape
    split_mesh = Mesh(
        mesh.devices.reshape(wide_size // 2, 2, narrow_size), (CHIPS, CORES, "narrow")
    )
    return jax.shard_map(
        on_device,
        mesh=split_mesh,
        in_specs=(
            P("narrow", WIDE),
            P(WIDE),
            P(None, None, WIDE, "narrow"),
            P(WIDE, "narrow", None),
            P("narrow", WIDE),
            P(WIDE, None, "narrow"),
            P("narrow", WIDE),
            P(WIDE),
            P(WIDE),
        ),
        out_specs=(P("narrow", WIDE), P(None, None, WIDE, "narrow")),
        check_vma=False,
    )
```

```python
import math

import jax
import jax.numpy as jnp
from jax import lax
from jax.sharding import Mesh
from jax.sharding import PartitionSpec as P

D = 8192
HD = 128
LAYERS = 2
CHIPS = "chips"
CORES = "cores"
WIDE = (CHIPS, CORES)


EPSILON = 1e-05
ROPE_BASE = 500000.0


def axis_length(axis):
    if isinstance(axis, tuple):
        return math.prod(lax.axis_size(name) for name in axis)
    return lax.axis_size(axis)


def swap_cores(shard):
    return lax.ppermute(shard, CORES, [(0, 1), (1, 0)])


def reduced_rows(partial, row_dim, wire_type):
    chips = lax.axis_size(CHIPS)
    shape = partial.shape
    split = shape[:row_dim] + (chips, 2, shape[row_dim] // (chips * 2)) + shape[row_dim + 1 :]
    blocks = partial.reshape(split)
    core = lax.axis_index(CORES)
    mine = lax.dynamic_index_in_dim(blocks, core, row_dim + 1, keepdims=False)
    other = lax.dynamic_index_in_dim(blocks, 1 - core, row_dim + 1, keepdims=False)
    pair_sum = mine.astype(jnp.float32) + swap_cores(other).astype(jnp.float32)
    return pair_sum, row_dim


def chip_sum(pair_sum, row_dim, wire_type):
    arrived = lax.all_to_all(pair_sum.astype(wire_type), CHIPS, row_dim, row_dim, tiled=True)
    return jnp.sum(arrived.astype(jnp.float32), axis=row_dim)


def gathered_rows_wide(shard):
    chips = lax.axis_size(CHIPS)
    from_chips = lax.all_to_all(
        jnp.broadcast_to(shard[None], (chips, *shard.shape)), CHIPS, 0, 0, tiled=True
    )
    from_partner = swap_cores(from_chips)
    first = lax.axis_index(CORES) == 0
    low_core = jnp.where(first, from_chips, from_partner)
    high_core = jnp.where(first, from_partner, from_chips)
    return jnp.stack([low_core, high_core], axis=1).reshape(-1, *shard.shape[1:])


def copy_for_each(shard, axis):
    length = axis_length(axis)
    return lax.all_to_all(
        jnp.broadcast_to(shard[None], (length, *shard.shape)), axis, 0, 0, tiled=True
    )


def of_everyone(shard, axis):
    return copy_for_each(shard, axis).sum(axis=0)


def laid_out(parts, dim):
    parts = jnp.moveaxis(parts, 0, dim)
    lengths = parts.shape
    return parts.reshape(*lengths[:dim], lengths[dim] * lengths[dim + 1], *lengths[dim + 2 :])


def gathered_copies(shard, axis, dim):
    parts = copy_for_each(shard, axis)
    return laid_out(parts, dim)


def in_blocks(shard, dim, length):
    before, after = (shard.shape[:dim], shard.shape[dim + 1 :])
    return jnp.moveaxis(shard.reshape(*before, length, -1, *after), dim, 0)


def summed_on_arrival(shard, axis, dim):
    parts = in_blocks(shard, dim, axis_length(axis))
    arrived = lax.all_to_all(parts, axis, split_axis=0, concat_axis=0, tiled=True)
    return arrived.sum(axis=0)


def sent_and_summed(shard, axis, dim):
    length = axis_length(axis)
    parts = lax.all_to_all(in_blocks(shard, dim, length), axis, 0, 0, tiled=True)
    return jnp.sum(parts.astype(jnp.float32), axis=0)


def scale_rows(floats, square_sum, gain):
    scaled = (
        floats * lax.rsqrt(square_sum / D + EPSILON)[:, None] * gain.astype(jnp.float32)[None, :]
    )
    return scaled.astype(jnp.bfloat16)


def norm_rows(stream, gain):
    floats = stream.astype(jnp.float32)
    square_sum = of_everyone(jnp.sum(floats * floats, axis=1), WIDE)
    return gathered_copies(scale_rows(floats, square_sum, gain), "narrow", 0)


def rotate_pairs(vectors, cosine, sine_table):
    half_dim = vectors.shape[-1] // 2
    first_half = vectors[..., :half_dim]
    second_half = vectors[..., half_dim:]
    return jnp.concatenate(
        [
            first_half * cosine - second_half * sine_table,
            second_half * cosine + first_half * sine_table,
        ],
        axis=-1,
    )


def rotary_tables(lengths, head_dim):
    half_dim = head_dim // 2
    inverse = jnp.exp(
        jnp.arange(half_dim, dtype=jnp.float32) * (-2.0 * math.log(ROPE_BASE) / head_dim)
    )
    angles = lengths.astype(jnp.float32)[:, None] * inverse[None, :]
    return (jnp.cos(angles), jnp.sin(angles))


def split_heads(projected, lengths, heads_kv, head_dim):
    row_count = projected.shape[0]
    grouped = projected.reshape(row_count, heads_kv, -1, head_dim)
    group_size = grouped.shape[2] - 2
    cosine, sine_table = rotary_tables(lengths, head_dim)
    rotated = rotate_pairs(
        grouped[:, :, : group_size + 1], cosine[:, None, None, :], sine_table[:, None, None, :]
    )
    queries = rotated[:, :, :group_size].astype(jnp.bfloat16)
    key_new = rotated[:, :, group_size].astype(jnp.bfloat16)
    value_new = grouped[:, :, group_size + 1].astype(jnp.bfloat16)
    return (queries, key_new, value_new)


def attend(queries, key_new, value_new, cached_keys, cached_values, lengths):
    row_count, heads_kv, group_size, head_dim = queries.shape
    slot_count = cached_keys.shape[0]
    score_scale = 1.0 / math.sqrt(head_dim)
    key_table = cached_keys.reshape(slot_count, heads_kv, head_dim)
    value_table = cached_values.reshape(slot_count, heads_kv, head_dim)
    starts = jnp.cumsum(lengths) - lengths
    position = jnp.arange(slot_count, dtype=jnp.int32)
    owned = (position[None, :] >= starts[:, None]) & (
        position[None, :] < (starts + lengths)[:, None]
    )
    scores = (
        jnp.einsum("rkgd,tkd->krgt", queries, key_table, preferred_element_type=jnp.float32)
        * score_scale
    )
    scores = jnp.where(owned[None, :, None, :], scores, -jnp.inf)
    own_score = (
        jnp.einsum("rkgd,rkd->krg", queries, key_new, preferred_element_type=jnp.float32)
        * score_scale
    )
    row_peak = jnp.maximum(jnp.max(scores, axis=3), own_score)
    weights = jnp.exp(scores - row_peak[..., None])
    own_weight = jnp.exp(own_score - row_peak)
    weight_sum = jnp.sum(weights, axis=3) + own_weight
    blended = jnp.einsum(
        "krgt,tkd->krgd",
        weights.astype(jnp.bfloat16),
        value_table,
        preferred_element_type=jnp.float32,
    )
    own_rounded = lax.optimization_barrier(own_weight.astype(jnp.bfloat16)).astype(jnp.float32)
    blended = blended + own_rounded[..., None] * jnp.transpose(value_new, (1, 0, 2))[
        :, :, None, :
    ].astype(jnp.float32)
    normalized = (blended / weight_sum[..., None]).astype(jnp.bfloat16)
    return jnp.transpose(normalized, (1, 0, 2, 3)).reshape(
        row_count, heads_kv * group_size * head_dim
    )


def split_hi_lo(values):
    high = values.astype(jnp.bfloat16)
    low = (values - high.astype(jnp.float32)).astype(jnp.bfloat16)
    return high, low


def gathered_rows(stream, gain):
    floats = stream.astype(jnp.float32)
    square_sum = jnp.sum(floats * floats, axis=1)
    scaled = (floats * gain.astype(jnp.float32)[None, :]).astype(jnp.bfloat16)
    high, low = split_hi_lo(square_sum)
    packed = jnp.concatenate([scaled, high[:, None], low[:, None]], axis=1)
    rows = gathered_copies(packed, "narrow", 0)
    width = stream.shape[1]
    partial_sum = rows[:, width].astype(jnp.float32) + rows[:, width + 1].astype(jnp.float32)
    return rows[:, :width], partial_sum


def row_scale(square_sum):
    return lax.rsqrt(square_sum / D + EPSILON)


def on_device(
    hidden_in, lengths, kv_cache, qkv_weight, o_weight, gate_up, down_weight, attn_gain, mlp_gain
):
    width_dev = hidden_in.shape[1]
    heads_kv = qkv_weight.shape[1]
    hidden_dev = down_weight.shape[0]
    flat_qkv = qkv_weight.reshape(width_dev, -1)
    stream = hidden_in
    entries = []
    for layer_index in range(LAYERS):
        if layer_index == 0:
            rows_in = norm_rows(stream, attn_gain)
            pair_sum, row_dim = reduced_rows(
                jnp.dot(rows_in, flat_qkv, preferred_element_type=jnp.float32), 0, jnp.float32
            )
            own_qkv = chip_sum(pair_sum, row_dim, jnp.float32)
        else:
            rows_in, partial_sum = gathered_rows(stream, attn_gain)
            projected = jnp.dot(rows_in, flat_qkv, preferred_element_type=jnp.float32)
            pair_sum, row_dim = reduced_rows(
                jnp.concatenate([projected, partial_sum[:, None]], axis=1), 0, jnp.float32
            )
            own = chip_sum(pair_sum, row_dim, jnp.float32)
            qkv_cols = flat_qkv.shape[1]
            own_qkv = own[:, :qkv_cols] * row_scale(own[:, qkv_cols])[:, None]
        queries, key_new, value_new = split_heads(own_qkv, lengths, heads_kv, HD)
        own_rows = key_new.shape[0]
        entries.append(
            jnp.stack(
                [
                    key_new.reshape(own_rows, heads_kv * HD),
                    value_new.reshape(own_rows, heads_kv * HD),
                ]
            )
        )
        attended = attend(
            queries, key_new, value_new, kv_cache[layer_index, 0], kv_cache[layer_index, 1], lengths
        )
        heads_all = gathered_rows_wide(attended)
        summed = summed_on_arrival(
            jnp.dot(heads_all, o_weight, preferred_element_type=jnp.float32), "narrow", 0
        )
        stream = (stream.astype(jnp.float32) + summed).astype(jnp.bfloat16)
        rows_in, partial_sum = gathered_rows(stream, mlp_gain)
        chips = lax.axis_size(CHIPS)
        core = lax.axis_index(CORES)
        by_core = rows_in.reshape(chips, 2, -1, rows_in.shape[1])
        sums_by_core = partial_sum.reshape(chips, 2, -1)
        reordered = jnp.concatenate(
            [
                lax.dynamic_index_in_dim(by_core, 1 - core, 1, keepdims=False),
                lax.dynamic_index_in_dim(by_core, core, 1, keepdims=False),
            ]
        ).reshape(rows_in.shape)
        reordered_sums = jnp.concatenate(
            [
                lax.dynamic_index_in_dim(sums_by_core, 1 - core, 1, keepdims=False),
                lax.dynamic_index_in_dim(sums_by_core, core, 1, keepdims=False),
            ]
        ).reshape(partial_sum.shape)
        both_parts = jnp.einsum(
            "rd,dkh->krh", reordered, gate_up, preferred_element_type=jnp.float32
        ).astype(jnp.bfloat16)
        high, low = split_hi_lo(reordered_sums)
        sums_col = jnp.stack([high, low])[:, :, None]
        payload = jnp.concatenate([both_parts, sums_col], axis=2)
        half = payload.shape[1] // 2
        block_shape = (2, chips, half // chips, hidden_dev + 1)
        to_partner = payload[:, :half].reshape(block_shape)
        kept = payload[:, half:].reshape(block_shape)
        from_partner = swap_cores(to_partner)
        pair_squares = (
            kept[0, :, :, hidden_dev].astype(jnp.float32)
            + kept[1, :, :, hidden_dev].astype(jnp.float32)
            + from_partner[0, :, :, hidden_dev].astype(jnp.float32)
            + from_partner[1, :, :, hidden_dev].astype(jnp.float32)
        )
        high, low = split_hi_lo(pair_squares)
        resplit = jnp.stack([high, low]).astype(jnp.float32)[..., None]
        column = lax.broadcasted_iota(jnp.int32, block_shape, 3)
        pair_sum = jnp.where(
            column == hidden_dev,
            resplit,
            kept.astype(jnp.float32) + from_partner.astype(jnp.float32),
        ).astype(jnp.bfloat16)
        own = chip_sum(pair_sum, 1, jnp.bfloat16)
        scale = row_scale(own[0, :, hidden_dev] + own[1, :, hidden_dev])[:, None]
        gate = own[0, :, :hidden_dev] * scale
        up = own[1, :, :hidden_dev] * scale
        activated = (jax.nn.silu(gate) * up).astype(jnp.bfloat16)
        partial_down = jnp.dot(
            gathered_rows_wide(activated), down_weight, preferred_element_type=jnp.float32
        )
        summed = summed_on_arrival(partial_down, "narrow", 0)
        stream = (stream.astype(jnp.float32) + summed).astype(jnp.bfloat16)
    return (stream, jnp.stack(entries))


def solution(mesh):
    wide_size, narrow_size = mesh.devices.shape
    split_mesh = Mesh(
        mesh.devices.reshape(wide_size // 2, 2, narrow_size), (CHIPS, CORES, "narrow")
    )
    return jax.shard_map(
        on_device,
        mesh=split_mesh,
        in_specs=(
            P("narrow", WIDE),
            P(WIDE),
            P(None, None, WIDE, "narrow"),
            P(WIDE, "narrow", None),
            P("narrow", WIDE),
            P(WIDE, None, "narrow"),
            P("narrow", WIDE),
            P(WIDE),
            P(WIDE),
        ),
        out_specs=(P("narrow", WIDE), P(None, None, WIDE, "narrow")),
        check_vma=False,
    )
```

```python
import math

import jax
import jax.numpy as jnp
from jax import lax
from jax.sharding import Mesh
from jax.sharding import PartitionSpec as P

D = 8192
HD = 128
LAYERS = 2
CHIPS = "chips"
CORES = "cores"
WIDE = (CHIPS, CORES)


EPSILON = 1e-05
ROPE_BASE = 500000.0


def axis_length(axis):
    if isinstance(axis, tuple):
        return math.prod(lax.axis_size(name) for name in axis)
    return lax.axis_size(axis)


def swap_cores(shard):
    return lax.ppermute(shard, CORES, [(0, 1), (1, 0)])


def reduced_rows(partial, row_dim, wire_type):
    chips = lax.axis_size(CHIPS)
    shape = partial.shape
    split = shape[:row_dim] + (chips, 2, shape[row_dim] // (chips * 2)) + shape[row_dim + 1 :]
    blocks = partial.reshape(split)
    core = lax.axis_index(CORES)
    mine = lax.dynamic_index_in_dim(blocks, core, row_dim + 1, keepdims=False)
    other = lax.dynamic_index_in_dim(blocks, 1 - core, row_dim + 1, keepdims=False)
    pair_sum = mine.astype(jnp.float32) + swap_cores(other).astype(jnp.float32)
    return pair_sum, row_dim


def chip_sum(pair_sum, row_dim, wire_type):
    arrived = lax.all_to_all(pair_sum.astype(wire_type), CHIPS, row_dim, row_dim, tiled=True)
    return jnp.sum(arrived.astype(jnp.float32), axis=row_dim)


def gathered_rows_wide(shard):
    chips = lax.axis_size(CHIPS)
    from_chips = lax.all_to_all(
        jnp.broadcast_to(shard[None], (chips, *shard.shape)), CHIPS, 0, 0, tiled=True
    )
    from_partner = swap_cores(from_chips)
    first = lax.axis_index(CORES) == 0
    low_core = jnp.where(first, from_chips, from_partner)
    high_core = jnp.where(first, from_partner, from_chips)
    return jnp.stack([low_core, high_core], axis=1).reshape(-1, *shard.shape[1:])


def copy_for_each(shard, axis):
    length = axis_length(axis)
    return lax.all_to_all(
        jnp.broadcast_to(shard[None], (length, *shard.shape)), axis, 0, 0, tiled=True
    )


def of_everyone(shard, axis):
    return copy_for_each(shard, axis).sum(axis=0)


def laid_out(parts, dim):
    parts = jnp.moveaxis(parts, 0, dim)
    lengths = parts.shape
    return parts.reshape(*lengths[:dim], lengths[dim] * lengths[dim + 1], *lengths[dim + 2 :])


def gathered_copies(shard, axis, dim):
    parts = copy_for_each(shard, axis)
    return laid_out(parts, dim)


def in_blocks(shard, dim, length):
    before, after = (shard.shape[:dim], shard.shape[dim + 1 :])
    return jnp.moveaxis(shard.reshape(*before, length, -1, *after), dim, 0)


def summed_on_arrival(shard, axis, dim):
    parts = in_blocks(shard, dim, axis_length(axis))
    arrived = lax.all_to_all(parts, axis, split_axis=0, concat_axis=0, tiled=True)
    return arrived.sum(axis=0)


def sent_and_summed(shard, axis, dim):
    length = axis_length(axis)
    parts = lax.all_to_all(in_blocks(shard, dim, length), axis, 0, 0, tiled=True)
    return jnp.sum(parts.astype(jnp.float32), axis=0)


def scale_rows(floats, square_sum, gain):
    scaled = (
        floats * lax.rsqrt(square_sum / D + EPSILON)[:, None] * gain.astype(jnp.float32)[None, :]
    )
    return scaled.astype(jnp.bfloat16)


def norm_rows(stream, gain):
    floats = stream.astype(jnp.float32)
    own_sum = jnp.sum(floats * floats, axis=1)
    square_sum = of_everyone(own_sum + swap_cores(own_sum), CHIPS)
    return gathered_copies(scale_rows(floats, square_sum, gain), "narrow", 0)


def rotate_pairs(vectors, cosine, sine_table):
    half_dim = vectors.shape[-1] // 2
    first_half = vectors[..., :half_dim]
    second_half = vectors[..., half_dim:]
    return jnp.concatenate(
        [
            first_half * cosine - second_half * sine_table,
            second_half * cosine + first_half * sine_table,
        ],
        axis=-1,
    )


def rotary_tables(lengths, head_dim):
    half_dim = head_dim // 2
    inverse = jnp.exp(
        jnp.arange(half_dim, dtype=jnp.float32) * (-2.0 * math.log(ROPE_BASE) / head_dim)
    )
    angles = lengths.astype(jnp.float32)[:, None] * inverse[None, :]
    return (jnp.cos(angles), jnp.sin(angles))


def split_heads(projected, lengths, heads_kv, head_dim):
    row_count = projected.shape[0]
    grouped = projected.reshape(row_count, heads_kv, -1, head_dim)
    group_size = grouped.shape[2] - 2
    cosine, sine_table = rotary_tables(lengths, head_dim)
    rotated = rotate_pairs(
        grouped[:, :, : group_size + 1], cosine[:, None, None, :], sine_table[:, None, None, :]
    )
    queries = rotated[:, :, :group_size].astype(jnp.bfloat16)
    key_new = rotated[:, :, group_size].astype(jnp.bfloat16)
    value_new = grouped[:, :, group_size + 1].astype(jnp.bfloat16)
    return (queries, key_new, value_new)


def attend(queries, key_new, value_new, cached_keys, cached_values, lengths):
    row_count, heads_kv, group_size, head_dim = queries.shape
    slot_count = cached_keys.shape[0]
    score_scale = 1.0 / math.sqrt(head_dim)
    key_table = cached_keys.reshape(slot_count, heads_kv, head_dim)
    value_table = cached_values.reshape(slot_count, heads_kv, head_dim)
    starts = jnp.cumsum(lengths) - lengths
    position = jnp.arange(slot_count, dtype=jnp.int32)
    owned = (position[None, :] >= starts[:, None]) & (
        position[None, :] < (starts + lengths)[:, None]
    )
    scores = (
        jnp.einsum("rkgd,tkd->krgt", queries, key_table, preferred_element_type=jnp.float32)
        * score_scale
    )
    scores = jnp.where(owned[None, :, None, :], scores, -jnp.inf)
    own_score = (
        jnp.einsum("rkgd,rkd->krg", queries, key_new, preferred_element_type=jnp.float32)
        * score_scale
    )
    row_peak = jnp.maximum(jnp.max(scores, axis=3), own_score)
    weights = jnp.exp(scores - row_peak[..., None])
    own_weight = jnp.exp(own_score - row_peak)
    weight_sum = jnp.sum(weights, axis=3) + own_weight
    blended = jnp.einsum(
        "krgt,tkd->krgd",
        weights.astype(jnp.bfloat16),
        value_table,
        preferred_element_type=jnp.float32,
    )
    own_rounded = lax.optimization_barrier(own_weight.astype(jnp.bfloat16)).astype(jnp.float32)
    blended = blended + own_rounded[..., None] * jnp.transpose(value_new, (1, 0, 2))[
        :, :, None, :
    ].astype(jnp.float32)
    normalized = (blended / weight_sum[..., None]).astype(jnp.bfloat16)
    return jnp.transpose(normalized, (1, 0, 2, 3)).reshape(
        row_count, heads_kv * group_size * head_dim
    )


def split_hi_lo(values):
    high = values.astype(jnp.bfloat16)
    low = (values - high.astype(jnp.float32)).astype(jnp.bfloat16)
    return high, low


def gathered_rows(stream, gain):
    floats = stream.astype(jnp.float32)
    square_sum = jnp.sum(floats * floats, axis=1)
    scaled = (floats * gain.astype(jnp.float32)[None, :]).astype(jnp.bfloat16)
    high, low = split_hi_lo(square_sum)
    packed = jnp.concatenate([scaled, high[:, None], low[:, None]], axis=1)
    rows = gathered_copies(packed, "narrow", 0)
    width = stream.shape[1]
    partial_sum = rows[:, width].astype(jnp.float32) + rows[:, width + 1].astype(jnp.float32)
    return rows[:, :width], partial_sum


def row_scale(square_sum):
    return lax.rsqrt(square_sum / D + EPSILON)


def on_device(
    hidden_in, lengths, kv_cache, qkv_weight, o_weight, gate_up, down_weight, attn_gain, mlp_gain
):
    width_dev = hidden_in.shape[1]
    heads_kv = qkv_weight.shape[1]
    hidden_dev = down_weight.shape[0]
    flat_qkv = qkv_weight.reshape(width_dev, -1)
    stream = hidden_in
    entries = []
    for layer_index in range(LAYERS):
        if layer_index == 0:
            rows_in = norm_rows(stream, attn_gain)
            pair_sum, row_dim = reduced_rows(
                jnp.dot(rows_in, flat_qkv, preferred_element_type=jnp.float32), 0, jnp.float32
            )
            own_qkv = chip_sum(pair_sum, row_dim, jnp.float32)
        else:
            rows_in, partial_sum = gathered_rows(stream, attn_gain)
            projected = jnp.dot(rows_in, flat_qkv, preferred_element_type=jnp.float32)
            pair_sum, row_dim = reduced_rows(
                jnp.concatenate([projected, partial_sum[:, None]], axis=1), 0, jnp.float32
            )
            own = chip_sum(pair_sum, row_dim, jnp.float32)
            qkv_cols = flat_qkv.shape[1]
            own_qkv = own[:, :qkv_cols] * row_scale(own[:, qkv_cols])[:, None]
        queries, key_new, value_new = split_heads(own_qkv, lengths, heads_kv, HD)
        own_rows = key_new.shape[0]
        entries.append(
            jnp.stack(
                [
                    key_new.reshape(own_rows, heads_kv * HD),
                    value_new.reshape(own_rows, heads_kv * HD),
                ]
            )
        )
        attended = attend(
            queries, key_new, value_new, kv_cache[layer_index, 0], kv_cache[layer_index, 1], lengths
        )
        heads_all = gathered_rows_wide(attended)
        summed = summed_on_arrival(
            jnp.dot(heads_all, o_weight, preferred_element_type=jnp.float32), "narrow", 0
        )
        stream = (stream.astype(jnp.float32) + summed).astype(jnp.bfloat16)
        rows_in, partial_sum = gathered_rows(stream, mlp_gain)
        chips = lax.axis_size(CHIPS)
        core = lax.axis_index(CORES)
        by_core = rows_in.reshape(chips, 2, -1, rows_in.shape[1])
        sums_by_core = partial_sum.reshape(chips, 2, -1)
        reordered = jnp.concatenate(
            [
                lax.dynamic_index_in_dim(by_core, 1 - core, 1, keepdims=False),
                lax.dynamic_index_in_dim(by_core, core, 1, keepdims=False),
            ]
        ).reshape(rows_in.shape)
        reordered_sums = jnp.concatenate(
            [
                lax.dynamic_index_in_dim(sums_by_core, 1 - core, 1, keepdims=False),
                lax.dynamic_index_in_dim(sums_by_core, core, 1, keepdims=False),
            ]
        ).reshape(partial_sum.shape)
        both_parts = jnp.einsum(
            "rd,dkh->krh", reordered, gate_up, preferred_element_type=jnp.float32
        ).astype(jnp.bfloat16)
        high, low = split_hi_lo(reordered_sums)
        sums_col = jnp.stack([high, low])[:, :, None]
        payload = jnp.concatenate([both_parts, sums_col], axis=2)
        half = payload.shape[1] // 2
        block_shape = (2, chips, half // chips, hidden_dev + 1)
        to_partner = payload[:, :half].reshape(block_shape)
        kept = payload[:, half:].reshape(block_shape)
        from_partner = swap_cores(to_partner)
        pair_squares = (
            kept[0, :, :, hidden_dev].astype(jnp.float32)
            + kept[1, :, :, hidden_dev].astype(jnp.float32)
            + from_partner[0, :, :, hidden_dev].astype(jnp.float32)
            + from_partner[1, :, :, hidden_dev].astype(jnp.float32)
        )
        high, low = split_hi_lo(pair_squares)
        resplit = jnp.stack([high, low]).astype(jnp.float32)[..., None]
        column = lax.broadcasted_iota(jnp.int32, block_shape, 3)
        pair_sum = jnp.where(
            column == hidden_dev,
            resplit,
            kept.astype(jnp.float32) + from_partner.astype(jnp.float32),
        ).astype(jnp.bfloat16)
        own = chip_sum(pair_sum, 1, jnp.bfloat16)
        scale = row_scale(own[0, :, hidden_dev] + own[1, :, hidden_dev])[:, None]
        gate = own[0, :, :hidden_dev] * scale
        up = own[1, :, :hidden_dev] * scale
        activated = (jax.nn.silu(gate) * up).astype(jnp.bfloat16)
        partial_down = jnp.dot(
            gathered_rows_wide(activated), down_weight, preferred_element_type=jnp.float32
        )
        summed = summed_on_arrival(partial_down, "narrow", 0)
        stream = (stream.astype(jnp.float32) + summed).astype(jnp.bfloat16)
    return (stream, jnp.stack(entries))


def solution(mesh):
    wide_size, narrow_size = mesh.devices.shape
    split_mesh = Mesh(
        mesh.devices.reshape(wide_size // 2, 2, narrow_size), (CHIPS, CORES, "narrow")
    )
    return jax.shard_map(
        on_device,
        mesh=split_mesh,
        in_specs=(
            P("narrow", WIDE),
            P(WIDE),
            P(None, None, WIDE, "narrow"),
            P(WIDE, "narrow", None),
            P("narrow", WIDE),
            P(WIDE, None, "narrow"),
            P("narrow", WIDE),
            P(WIDE),
            P(WIDE),
        ),
        out_specs=(P("narrow", WIDE), P(None, None, WIDE, "narrow")),
        check_vma=False,
    )
```

```python
import math

import jax
import jax.numpy as jnp
from jax import lax
from jax.experimental import pallas as pl
from jax.sharding import Mesh
from jax.sharding import PartitionSpec as P

D = 8192
HD = 128
LAYERS = 2
CHIPS = "chips"
CORES = "cores"
WIDE = (CHIPS, CORES)


EPSILON = 1e-05
ROPE_BASE = 500000.0


def axis_length(axis):
    if isinstance(axis, tuple):
        return math.prod(lax.axis_size(name) for name in axis)
    return lax.axis_size(axis)


def swap_cores(shard):
    return lax.ppermute(shard, CORES, [(0, 1), (1, 0)])


def reduced_rows(partial, row_dim, wire_type):
    chips = lax.axis_size(CHIPS)
    shape = partial.shape
    split = shape[:row_dim] + (chips, 2, shape[row_dim] // (chips * 2)) + shape[row_dim + 1 :]
    blocks = partial.reshape(split)
    core = lax.axis_index(CORES)
    mine = lax.dynamic_index_in_dim(blocks, core, row_dim + 1, keepdims=False)
    other = lax.dynamic_index_in_dim(blocks, 1 - core, row_dim + 1, keepdims=False)
    pair_sum = mine.astype(jnp.float32) + swap_cores(other).astype(jnp.float32)
    return pair_sum, row_dim


def chip_sum(pair_sum, row_dim, wire_type):
    arrived = lax.all_to_all(pair_sum.astype(wire_type), CHIPS, row_dim, row_dim, tiled=True)
    return jnp.sum(arrived.astype(jnp.float32), axis=row_dim)


def gathered_rows_wide(shard):
    chips = lax.axis_size(CHIPS)
    from_chips = lax.all_to_all(
        jnp.broadcast_to(shard[None], (chips, *shard.shape)), CHIPS, 0, 0, tiled=True
    )
    from_partner = swap_cores(from_chips)
    first = lax.axis_index(CORES) == 0
    low_core = jnp.where(first, from_chips, from_partner)
    high_core = jnp.where(first, from_partner, from_chips)
    return jnp.stack([low_core, high_core], axis=1).reshape(-1, *shard.shape[1:])


def copy_for_each(shard, axis):
    length = axis_length(axis)
    return lax.all_to_all(
        jnp.broadcast_to(shard[None], (length, *shard.shape)), axis, 0, 0, tiled=True
    )


def of_everyone(shard, axis):
    return copy_for_each(shard, axis).sum(axis=0)


def laid_out(parts, dim):
    parts = jnp.moveaxis(parts, 0, dim)
    lengths = parts.shape
    return parts.reshape(*lengths[:dim], lengths[dim] * lengths[dim + 1], *lengths[dim + 2 :])


def gathered_copies(shard, axis, dim):
    parts = copy_for_each(shard, axis)
    return laid_out(parts, dim)


def in_blocks(shard, dim, length):
    before, after = (shard.shape[:dim], shard.shape[dim + 1 :])
    return jnp.moveaxis(shard.reshape(*before, length, -1, *after), dim, 0)


def summed_on_arrival(shard, axis, dim):
    parts = in_blocks(shard, dim, axis_length(axis))
    arrived = lax.all_to_all(parts, axis, split_axis=0, concat_axis=0, tiled=True)
    return arrived.sum(axis=0)


def sent_and_summed(shard, axis, dim):
    length = axis_length(axis)
    parts = lax.all_to_all(in_blocks(shard, dim, length), axis, 0, 0, tiled=True)
    return jnp.sum(parts.astype(jnp.float32), axis=0)


def scale_rows(floats, square_sum, gain):
    scaled = (
        floats * lax.rsqrt(square_sum / D + EPSILON)[:, None] * gain.astype(jnp.float32)[None, :]
    )
    return scaled.astype(jnp.bfloat16)


def norm_rows(stream, gain):
    floats = stream.astype(jnp.float32)
    square_sum = of_everyone(jnp.sum(floats * floats, axis=1), WIDE)
    return gathered_copies(scale_rows(floats, square_sum, gain), "narrow", 0)


def rotate_pairs(vectors, cosine, sine_table):
    half_dim = vectors.shape[-1] // 2
    first_half = vectors[..., :half_dim]
    second_half = vectors[..., half_dim:]
    return jnp.concatenate(
        [
            first_half * cosine - second_half * sine_table,
            second_half * cosine + first_half * sine_table,
        ],
        axis=-1,
    )


def rotary_tables(lengths, head_dim):
    half_dim = head_dim // 2
    inverse = jnp.exp(
        jnp.arange(half_dim, dtype=jnp.float32) * (-2.0 * math.log(ROPE_BASE) / head_dim)
    )
    angles = lengths.astype(jnp.float32)[:, None] * inverse[None, :]
    return (jnp.cos(angles), jnp.sin(angles))


def split_heads(projected, lengths, heads_kv, head_dim):
    row_count = projected.shape[0]
    grouped = projected.reshape(row_count, heads_kv, -1, head_dim)
    group_size = grouped.shape[2] - 2
    cosine, sine_table = rotary_tables(lengths, head_dim)
    rotated = rotate_pairs(
        grouped[:, :, : group_size + 1], cosine[:, None, None, :], sine_table[:, None, None, :]
    )
    queries = rotated[:, :, :group_size].astype(jnp.bfloat16)
    key_new = rotated[:, :, group_size].astype(jnp.bfloat16)
    value_new = grouped[:, :, group_size + 1].astype(jnp.bfloat16)
    return (queries, key_new, value_new)


def attend(queries, key_new, value_new, cached_keys, cached_values, lengths):
    row_count, heads_kv, group_size, head_dim = queries.shape
    slot_count = cached_keys.shape[0]
    score_scale = 1.0 / math.sqrt(head_dim)
    key_table = cached_keys.reshape(slot_count, heads_kv, head_dim)
    value_table = cached_values.reshape(slot_count, heads_kv, head_dim)
    starts = jnp.cumsum(lengths) - lengths
    position = jnp.arange(slot_count, dtype=jnp.int32)
    owned = (position[None, :] >= starts[:, None]) & (
        position[None, :] < (starts + lengths)[:, None]
    )
    scores = (
        jnp.einsum("rkgd,tkd->krgt", queries, key_table, preferred_element_type=jnp.float32)
        * score_scale
    )
    scores = jnp.where(owned[None, :, None, :], scores, -jnp.inf)
    own_score = (
        jnp.einsum("rkgd,rkd->krg", queries, key_new, preferred_element_type=jnp.float32)
        * score_scale
    )
    row_peak = jnp.maximum(jnp.max(scores, axis=3), own_score)
    weights = jnp.exp(scores - row_peak[..., None])
    own_weight = jnp.exp(own_score - row_peak)
    weight_sum = jnp.sum(weights, axis=3) + own_weight
    blended = jnp.einsum(
        "krgt,tkd->krgd",
        weights.astype(jnp.bfloat16),
        value_table,
        preferred_element_type=jnp.float32,
    )
    own_rounded = lax.optimization_barrier(own_weight.astype(jnp.bfloat16)).astype(jnp.float32)
    blended = blended + own_rounded[..., None] * jnp.transpose(value_new, (1, 0, 2))[
        :, :, None, :
    ].astype(jnp.float32)
    normalized = (blended / weight_sum[..., None]).astype(jnp.bfloat16)
    return jnp.transpose(normalized, (1, 0, 2, 3)).reshape(
        row_count, heads_kv * group_size * head_dim
    )


def attention_kernel(q_ref, kn_ref, vn_ref, lo_ref, hi_ref, k_ref, v_ref, out_ref):
    score_scale = 1.0 / math.sqrt(HD)
    queries = q_ref[...]
    keys = k_ref[...]
    scores = lax.dot_general(
        queries, keys, (((1,), (1,)), ((), ())), preferred_element_type=jnp.float32
    ) * score_scale
    position = lax.broadcasted_iota(jnp.int32, scores.shape, 1)
    owned = (position >= lo_ref[...]) & (position < hi_ref[...])
    scores = jnp.where(owned, scores, -jnp.inf)
    query_floats = queries.astype(jnp.float32)
    own_score = (
        jnp.sum(query_floats * kn_ref[...].astype(jnp.float32), axis=1, keepdims=True)
        * score_scale
    )
    peak = jnp.maximum(jnp.max(scores, axis=1, keepdims=True), own_score)
    weights = jnp.exp(scores - peak)
    own_weight = jnp.exp(own_score - peak)
    weight_sum = jnp.sum(weights, axis=1, keepdims=True) + own_weight
    blended = jnp.dot(
        weights.astype(jnp.bfloat16), v_ref[...], preferred_element_type=jnp.float32
    )
    own_rounded = own_weight.astype(jnp.bfloat16).astype(jnp.float32)
    blended = blended + own_rounded * vn_ref[...].astype(jnp.float32)
    out_ref[...] = (blended / weight_sum).astype(out_ref.dtype)


def attend_kernel(queries, key_new, value_new, kv_cache, layer_index, lengths):
    row_count, heads_kv, group_size, head_dim = queries.shape
    slot_count = kv_cache.shape[2]
    rows = row_count * group_size
    starts = jnp.cumsum(lengths) - lengths
    lo = jnp.repeat(starts, group_size)[:, None].astype(jnp.int32)
    hi = jnp.repeat(starts + lengths, group_size)[:, None].astype(jnp.int32)
    q_rows = queries.reshape(rows, head_dim)
    kn_rows = jnp.repeat(key_new.reshape(row_count, head_dim), group_size, axis=0)
    vn_rows = jnp.repeat(value_new.reshape(row_count, head_dim), group_size, axis=0)
    whole = lambda shape: pl.BlockSpec(shape, lambda i: (0,) * len(shape))
    cache_spec = lambda which: pl.BlockSpec(
        (None, None, slot_count, head_dim), lambda i: (layer_index, which, 0, 0)
    )
    out = pl.pallas_call(
        attention_kernel,
        grid=(1,),
        in_specs=[
            whole((rows, head_dim)),
            whole((rows, head_dim)),
            whole((rows, head_dim)),
            whole((rows, 1)),
            whole((rows, 1)),
            cache_spec(0),
            cache_spec(1),
        ],
        out_specs=whole((rows, head_dim)),
        out_shape=jax.ShapeDtypeStruct((rows, head_dim), jnp.bfloat16),
    )(q_rows, kn_rows, vn_rows, lo, hi, kv_cache, kv_cache)
    return out.reshape(row_count, heads_kv * group_size * head_dim)


def split_hi_lo(values):
    high = values.astype(jnp.bfloat16)
    low = (values - high.astype(jnp.float32)).astype(jnp.bfloat16)
    return high, low


def gathered_rows(stream, gain):
    floats = stream.astype(jnp.float32)
    square_sum = jnp.sum(floats * floats, axis=1)
    scaled = (floats * gain.astype(jnp.float32)[None, :]).astype(jnp.bfloat16)
    high, low = split_hi_lo(square_sum)
    packed = jnp.concatenate([scaled, high[:, None], low[:, None]], axis=1)
    rows = gathered_copies(packed, "narrow", 0)
    width = stream.shape[1]
    partial_sum = rows[:, width].astype(jnp.float32) + rows[:, width + 1].astype(jnp.float32)
    return rows[:, :width], partial_sum


def row_scale(square_sum):
    return lax.rsqrt(square_sum / D + EPSILON)


def on_device(
    hidden_in, lengths, kv_cache, qkv_weight, o_weight, gate_up, down_weight, attn_gain, mlp_gain
):
    width_dev = hidden_in.shape[1]
    heads_kv = qkv_weight.shape[1]
    hidden_dev = down_weight.shape[0]
    flat_qkv = qkv_weight.reshape(width_dev, -1)
    stream = hidden_in
    entries = []
    for layer_index in range(LAYERS):
        if layer_index == 0:
            rows_in = norm_rows(stream, attn_gain)
            pair_sum, row_dim = reduced_rows(
                jnp.dot(rows_in, flat_qkv, preferred_element_type=jnp.float32), 0, jnp.float32
            )
            own_qkv = chip_sum(pair_sum, row_dim, jnp.float32)
        else:
            rows_in, partial_sum = gathered_rows(stream, attn_gain)
            projected = jnp.dot(rows_in, flat_qkv, preferred_element_type=jnp.float32)
            pair_sum, row_dim = reduced_rows(
                jnp.concatenate([projected, partial_sum[:, None]], axis=1), 0, jnp.float32
            )
            own = chip_sum(pair_sum, row_dim, jnp.float32)
            qkv_cols = flat_qkv.shape[1]
            own_qkv = own[:, :qkv_cols] * row_scale(own[:, qkv_cols])[:, None]
        queries, key_new, value_new = split_heads(own_qkv, lengths, heads_kv, HD)
        own_rows = key_new.shape[0]
        entries.append(
            jnp.stack(
                [
                    key_new.reshape(own_rows, heads_kv * HD),
                    value_new.reshape(own_rows, heads_kv * HD),
                ]
            )
        )
        attended = attend_kernel(queries, key_new, value_new, kv_cache, layer_index, lengths)
        heads_all = gathered_rows_wide(attended)
        summed = summed_on_arrival(
            jnp.dot(heads_all, o_weight, preferred_element_type=jnp.float32), "narrow", 0
        )
        stream = (stream.astype(jnp.float32) + summed).astype(jnp.bfloat16)
        rows_in, partial_sum = gathered_rows(stream, mlp_gain)
        chips = lax.axis_size(CHIPS)
        core = lax.axis_index(CORES)
        by_core = rows_in.reshape(chips, 2, -1, rows_in.shape[1])
        sums_by_core = partial_sum.reshape(chips, 2, -1)
        reordered = jnp.concatenate(
            [
                lax.dynamic_index_in_dim(by_core, 1 - core, 1, keepdims=False),
                lax.dynamic_index_in_dim(by_core, core, 1, keepdims=False),
            ]
        ).reshape(rows_in.shape)
        reordered_sums = jnp.concatenate(
            [
                lax.dynamic_index_in_dim(sums_by_core, 1 - core, 1, keepdims=False),
                lax.dynamic_index_in_dim(sums_by_core, core, 1, keepdims=False),
            ]
        ).reshape(partial_sum.shape)
        both_parts = jnp.einsum(
            "rd,dkh->krh", reordered, gate_up, preferred_element_type=jnp.float32
        ).astype(jnp.bfloat16)
        high, low = split_hi_lo(reordered_sums)
        sums_col = jnp.stack([high, low])[:, :, None]
        payload = jnp.concatenate([both_parts, sums_col], axis=2)
        half = payload.shape[1] // 2
        block_shape = (2, chips, half // chips, hidden_dev + 1)
        to_partner = payload[:, :half].reshape(block_shape)
        kept = payload[:, half:].reshape(block_shape)
        from_partner = swap_cores(to_partner)
        pair_squares = (
            kept[0, :, :, hidden_dev].astype(jnp.float32)
            + kept[1, :, :, hidden_dev].astype(jnp.float32)
            + from_partner[0, :, :, hidden_dev].astype(jnp.float32)
            + from_partner[1, :, :, hidden_dev].astype(jnp.float32)
        )
        high, low = split_hi_lo(pair_squares)
        resplit = jnp.stack([high, low]).astype(jnp.float32)[..., None]
        column = lax.broadcasted_iota(jnp.int32, block_shape, 3)
        pair_sum = jnp.where(
            column == hidden_dev,
            resplit,
            kept.astype(jnp.float32) + from_partner.astype(jnp.float32),
        ).astype(jnp.bfloat16)
        own = chip_sum(pair_sum, 1, jnp.bfloat16)
        scale = row_scale(own[0, :, hidden_dev] + own[1, :, hidden_dev])[:, None]
        gate = own[0, :, :hidden_dev] * scale
        up = own[1, :, :hidden_dev] * scale
        activated = (jax.nn.silu(gate) * up).astype(jnp.bfloat16)
        partial_down = jnp.dot(
            gathered_rows_wide(activated), down_weight, preferred_element_type=jnp.float32
        )
        summed = summed_on_arrival(partial_down, "narrow", 0)
        stream = (stream.astype(jnp.float32) + summed).astype(jnp.bfloat16)
    return (stream, jnp.stack(entries))


def solution(mesh):
    wide_size, narrow_size = mesh.devices.shape
    split_mesh = Mesh(
        mesh.devices.reshape(wide_size // 2, 2, narrow_size), (CHIPS, CORES, "narrow")
    )
    return jax.shard_map(
        on_device,
        mesh=split_mesh,
        in_specs=(
            P("narrow", WIDE),
            P(WIDE),
            P(None, None, WIDE, "narrow"),
            P(WIDE, "narrow", None),
            P("narrow", WIDE),
            P(WIDE, None, "narrow"),
            P("narrow", WIDE),
            P(WIDE),
            P(WIDE),
        ),
        out_specs=(P("narrow", WIDE), P(None, None, WIDE, "narrow")),
        check_vma=False,
    )
```

```python
import math

import jax
import jax.numpy as jnp
from jax import lax
from jax.sharding import Mesh
from jax.sharding import PartitionSpec as P

D = 8192
HD = 128
LAYERS = 2
CHIPS = "chips"
CORES = "cores"
WIDE = (CHIPS, CORES)


EPSILON = 1e-05
ROPE_BASE = 500000.0


def axis_length(axis):
    if isinstance(axis, tuple):
        return math.prod(lax.axis_size(name) for name in axis)
    return lax.axis_size(axis)


def swap_cores(shard):
    return lax.ppermute(shard, CORES, [(0, 1), (1, 0)])


def reduced_rows(partial, row_dim, wire_type):
    chips = lax.axis_size(CHIPS)
    shape = partial.shape
    split = shape[:row_dim] + (chips, 2, shape[row_dim] // (chips * 2)) + shape[row_dim + 1 :]
    blocks = partial.reshape(split)
    core = lax.axis_index(CORES)
    mine = lax.dynamic_index_in_dim(blocks, core, row_dim + 1, keepdims=False)
    other = lax.dynamic_index_in_dim(blocks, 1 - core, row_dim + 1, keepdims=False)
    pair_sum = mine.astype(jnp.float32) + swap_cores(other).astype(jnp.float32)
    return pair_sum, row_dim


def chip_sum(pair_sum, row_dim, wire_type):
    arrived = lax.all_to_all(pair_sum.astype(wire_type), CHIPS, row_dim, row_dim, tiled=True)
    return jnp.sum(arrived.astype(jnp.float32), axis=row_dim)


def gathered_rows_wide(shard):
    chips = lax.axis_size(CHIPS)
    from_chips = lax.all_to_all(
        jnp.broadcast_to(shard[None], (chips, *shard.shape)), CHIPS, 0, 0, tiled=True
    )
    from_partner = swap_cores(from_chips)
    first = lax.axis_index(CORES) == 0
    low_core = jnp.where(first, from_chips, from_partner)
    high_core = jnp.where(first, from_partner, from_chips)
    return jnp.stack([low_core, high_core], axis=1).reshape(-1, *shard.shape[1:])


def gathered_product(shard, weight):
    chips = lax.axis_size(CHIPS)
    from_chips = lax.all_to_all(
        jnp.broadcast_to(shard[None], (chips, *shard.shape)), CHIPS, 0, 0, tiled=True
    )
    from_partner = swap_cores(from_chips)
    mine = jnp.dot(
        from_chips.reshape(-1, shard.shape[1]), weight, preferred_element_type=jnp.float32
    )
    other = jnp.dot(
        from_partner.reshape(-1, shard.shape[1]), weight, preferred_element_type=jnp.float32
    )
    mine = mine.reshape(chips, -1, weight.shape[1])
    other = other.reshape(chips, -1, weight.shape[1])
    first = lax.axis_index(CORES) == 0
    low_core = jnp.where(first, mine, other)
    high_core = jnp.where(first, other, mine)
    return jnp.stack([low_core, high_core], axis=1).reshape(-1, weight.shape[1])


def copy_for_each(shard, axis):
    length = axis_length(axis)
    return lax.all_to_all(
        jnp.broadcast_to(shard[None], (length, *shard.shape)), axis, 0, 0, tiled=True
    )


def of_everyone(shard, axis):
    return copy_for_each(shard, axis).sum(axis=0)


def laid_out(parts, dim):
    parts = jnp.moveaxis(parts, 0, dim)
    lengths = parts.shape
    return parts.reshape(*lengths[:dim], lengths[dim] * lengths[dim + 1], *lengths[dim + 2 :])


def gathered_copies(shard, axis, dim):
    parts = copy_for_each(shard, axis)
    return laid_out(parts, dim)


def in_blocks(shard, dim, length):
    before, after = (shard.shape[:dim], shard.shape[dim + 1 :])
    return jnp.moveaxis(shard.reshape(*before, length, -1, *after), dim, 0)


def summed_on_arrival(shard, axis, dim):
    parts = in_blocks(shard, dim, axis_length(axis))
    arrived = lax.all_to_all(parts, axis, split_axis=0, concat_axis=0, tiled=True)
    return arrived.sum(axis=0)


def sent_and_summed(shard, axis, dim):
    length = axis_length(axis)
    parts = lax.all_to_all(in_blocks(shard, dim, length), axis, 0, 0, tiled=True)
    return jnp.sum(parts.astype(jnp.float32), axis=0)


def scale_rows(floats, square_sum, gain):
    scaled = (
        floats * lax.rsqrt(square_sum / D + EPSILON)[:, None] * gain.astype(jnp.float32)[None, :]
    )
    return scaled.astype(jnp.bfloat16)


def norm_rows(stream, gain):
    floats = stream.astype(jnp.float32)
    square_sum = of_everyone(jnp.sum(floats * floats, axis=1), WIDE)
    return gathered_copies(scale_rows(floats, square_sum, gain), "narrow", 0)


def rotate_pairs(vectors, cosine, sine_table):
    half_dim = vectors.shape[-1] // 2
    first_half = vectors[..., :half_dim]
    second_half = vectors[..., half_dim:]
    return jnp.concatenate(
        [
            first_half * cosine - second_half * sine_table,
            second_half * cosine + first_half * sine_table,
        ],
        axis=-1,
    )


def rotary_tables(lengths, head_dim):
    half_dim = head_dim // 2
    inverse = jnp.exp(
        jnp.arange(half_dim, dtype=jnp.float32) * (-2.0 * math.log(ROPE_BASE) / head_dim)
    )
    angles = lengths.astype(jnp.float32)[:, None] * inverse[None, :]
    return (jnp.cos(angles), jnp.sin(angles))


def split_heads(projected, lengths, heads_kv, head_dim):
    row_count = projected.shape[0]
    grouped = projected.reshape(row_count, heads_kv, -1, head_dim)
    group_size = grouped.shape[2] - 2
    cosine, sine_table = rotary_tables(lengths, head_dim)
    rotated = rotate_pairs(
        grouped[:, :, : group_size + 1], cosine[:, None, None, :], sine_table[:, None, None, :]
    )
    queries = rotated[:, :, :group_size].astype(jnp.bfloat16)
    key_new = rotated[:, :, group_size].astype(jnp.bfloat16)
    value_new = grouped[:, :, group_size + 1].astype(jnp.bfloat16)
    return (queries, key_new, value_new)


def attend(queries, key_new, value_new, cached_keys, cached_values, lengths):
    row_count, heads_kv, group_size, head_dim = queries.shape
    slot_count = cached_keys.shape[0]
    score_scale = 1.0 / math.sqrt(head_dim)
    key_table = cached_keys.reshape(slot_count, heads_kv, head_dim)
    value_table = cached_values.reshape(slot_count, heads_kv, head_dim)
    starts = jnp.cumsum(lengths) - lengths
    position = jnp.arange(slot_count, dtype=jnp.int32)
    owned = (position[None, :] >= starts[:, None]) & (
        position[None, :] < (starts + lengths)[:, None]
    )
    scores = (
        jnp.einsum("rkgd,tkd->krgt", queries, key_table, preferred_element_type=jnp.float32)
        * score_scale
    )
    scores = jnp.where(owned[None, :, None, :], scores, -jnp.inf)
    own_score = (
        jnp.einsum("rkgd,rkd->krg", queries, key_new, preferred_element_type=jnp.float32)
        * score_scale
    )
    row_peak = jnp.maximum(jnp.max(scores, axis=3), own_score)
    weights = jnp.exp(scores - row_peak[..., None])
    own_weight = jnp.exp(own_score - row_peak)
    weight_sum = jnp.sum(weights, axis=3) + own_weight
    blended = jnp.einsum(
        "krgt,tkd->krgd",
        weights.astype(jnp.bfloat16),
        value_table,
        preferred_element_type=jnp.float32,
    )
    own_rounded = lax.optimization_barrier(own_weight.astype(jnp.bfloat16)).astype(jnp.float32)
    blended = blended + own_rounded[..., None] * jnp.transpose(value_new, (1, 0, 2))[
        :, :, None, :
    ].astype(jnp.float32)
    normalized = (blended / weight_sum[..., None]).astype(jnp.bfloat16)
    return jnp.transpose(normalized, (1, 0, 2, 3)).reshape(
        row_count, heads_kv * group_size * head_dim
    )


def split_hi_lo(values):
    high = values.astype(jnp.bfloat16)
    low = (values - high.astype(jnp.float32)).astype(jnp.bfloat16)
    return high, low


def gathered_rows(stream, gain):
    floats = stream.astype(jnp.float32)
    square_sum = jnp.sum(floats * floats, axis=1)
    scaled = (floats * gain.astype(jnp.float32)[None, :]).astype(jnp.bfloat16)
    high, low = split_hi_lo(square_sum)
    packed = jnp.concatenate([scaled, high[:, None], low[:, None]], axis=1)
    rows = gathered_copies(packed, "narrow", 0)
    width = stream.shape[1]
    partial_sum = rows[:, width].astype(jnp.float32) + rows[:, width + 1].astype(jnp.float32)
    return rows[:, :width], partial_sum


def row_scale(square_sum):
    return lax.rsqrt(square_sum / D + EPSILON)


def on_device(
    hidden_in, lengths, kv_cache, qkv_weight, o_weight, gate_up, down_weight, attn_gain, mlp_gain
):
    width_dev = hidden_in.shape[1]
    heads_kv = qkv_weight.shape[1]
    hidden_dev = down_weight.shape[0]
    flat_qkv = qkv_weight.reshape(width_dev, -1)
    stream = hidden_in
    entries = []
    for layer_index in range(LAYERS):
        if layer_index == 0:
            rows_in = norm_rows(stream, attn_gain)
            pair_sum, row_dim = reduced_rows(
                jnp.dot(rows_in, flat_qkv, preferred_element_type=jnp.float32), 0, jnp.float32
            )
            own_qkv = chip_sum(pair_sum, row_dim, jnp.float32)
        else:
            rows_in, partial_sum = gathered_rows(stream, attn_gain)
            projected = jnp.dot(rows_in, flat_qkv, preferred_element_type=jnp.float32)
            pair_sum, row_dim = reduced_rows(
                jnp.concatenate([projected, partial_sum[:, None]], axis=1), 0, jnp.float32
            )
            own = chip_sum(pair_sum, row_dim, jnp.float32)
            qkv_cols = flat_qkv.shape[1]
            own_qkv = own[:, :qkv_cols] * row_scale(own[:, qkv_cols])[:, None]
        queries, key_new, value_new = split_heads(own_qkv, lengths, heads_kv, HD)
        own_rows = key_new.shape[0]
        entries.append(
            jnp.stack(
                [
                    key_new.reshape(own_rows, heads_kv * HD),
                    value_new.reshape(own_rows, heads_kv * HD),
                ]
            )
        )
        attended = attend(
            queries, key_new, value_new, kv_cache[layer_index, 0], kv_cache[layer_index, 1], lengths
        )
        summed = summed_on_arrival(gathered_product(attended, o_weight), "narrow", 0)
        stream = (stream.astype(jnp.float32) + summed).astype(jnp.bfloat16)
        rows_in, partial_sum = gathered_rows(stream, mlp_gain)
        chips = lax.axis_size(CHIPS)
        core = lax.axis_index(CORES)
        by_core = rows_in.reshape(chips, 2, -1, rows_in.shape[1])
        sums_by_core = partial_sum.reshape(chips, 2, -1)
        reordered = jnp.concatenate(
            [
                lax.dynamic_index_in_dim(by_core, 1 - core, 1, keepdims=False),
                lax.dynamic_index_in_dim(by_core, core, 1, keepdims=False),
            ]
        ).reshape(rows_in.shape)
        reordered_sums = jnp.concatenate(
            [
                lax.dynamic_index_in_dim(sums_by_core, 1 - core, 1, keepdims=False),
                lax.dynamic_index_in_dim(sums_by_core, core, 1, keepdims=False),
            ]
        ).reshape(partial_sum.shape)
        both_parts = jnp.einsum(
            "rd,dkh->krh", reordered, gate_up, preferred_element_type=jnp.float32
        ).astype(jnp.bfloat16)
        high, low = split_hi_lo(reordered_sums)
        sums_col = jnp.stack([high, low])[:, :, None]
        payload = jnp.concatenate([both_parts, sums_col], axis=2)
        half = payload.shape[1] // 2
        block_shape = (2, chips, half // chips, hidden_dev + 1)
        to_partner = payload[:, :half].reshape(block_shape)
        kept = payload[:, half:].reshape(block_shape)
        from_partner = swap_cores(to_partner)
        pair_squares = (
            kept[0, :, :, hidden_dev].astype(jnp.float32)
            + kept[1, :, :, hidden_dev].astype(jnp.float32)
            + from_partner[0, :, :, hidden_dev].astype(jnp.float32)
            + from_partner[1, :, :, hidden_dev].astype(jnp.float32)
        )
        high, low = split_hi_lo(pair_squares)
        resplit = jnp.stack([high, low]).astype(jnp.float32)[..., None]
        column = lax.broadcasted_iota(jnp.int32, block_shape, 3)
        pair_sum = jnp.where(
            column == hidden_dev,
            resplit,
            kept.astype(jnp.float32) + from_partner.astype(jnp.float32),
        ).astype(jnp.bfloat16)
        own = chip_sum(pair_sum, 1, jnp.bfloat16)
        scale = row_scale(own[0, :, hidden_dev] + own[1, :, hidden_dev])[:, None]
        gate = own[0, :, :hidden_dev] * scale
        up = own[1, :, :hidden_dev] * scale
        activated = (jax.nn.silu(gate) * up).astype(jnp.bfloat16)
        partial_down = gathered_product(activated, down_weight)
        summed = summed_on_arrival(partial_down, "narrow", 0)
        stream = (stream.astype(jnp.float32) + summed).astype(jnp.bfloat16)
    return (stream, jnp.stack(entries))


def solution(mesh):
    wide_size, narrow_size = mesh.devices.shape
    split_mesh = Mesh(
        mesh.devices.reshape(wide_size // 2, 2, narrow_size), (CHIPS, CORES, "narrow")
    )
    return jax.shard_map(
        on_device,
        mesh=split_mesh,
        in_specs=(
            P("narrow", WIDE),
            P(WIDE),
            P(None, None, WIDE, "narrow"),
            P(WIDE, "narrow", None),
            P("narrow", WIDE),
            P(WIDE, None, "narrow"),
            P("narrow", WIDE),
            P(WIDE),
            P(WIDE),
        ),
        out_specs=(P("narrow", WIDE), P(None, None, WIDE, "narrow")),
        check_vma=False,
    )
```

```python
import math

import jax
import jax.numpy as jnp
from jax import lax
from jax.sharding import Mesh
from jax.sharding import PartitionSpec as P

D = 8192
HD = 128
LAYERS = 2
CHIPS = "chips"
CORES = "cores"
WIDE = (CHIPS, CORES)


EPSILON = 1e-05
ROPE_BASE = 500000.0


def axis_length(axis):
    if isinstance(axis, tuple):
        return math.prod(lax.axis_size(name) for name in axis)
    return lax.axis_size(axis)


def swap_cores(shard):
    return lax.ppermute(shard, CORES, [(0, 1), (1, 0)])


def reduced_rows(partial, row_dim, wire_type):
    chips = lax.axis_size(CHIPS)
    shape = partial.shape
    split = shape[:row_dim] + (chips, 2, shape[row_dim] // (chips * 2)) + shape[row_dim + 1 :]
    blocks = partial.reshape(split)
    core = lax.axis_index(CORES)
    mine = lax.dynamic_index_in_dim(blocks, core, row_dim + 1, keepdims=False)
    other = lax.dynamic_index_in_dim(blocks, 1 - core, row_dim + 1, keepdims=False)
    pair_sum = mine.astype(jnp.float32) + swap_cores(other).astype(jnp.float32)
    return pair_sum, row_dim


def chip_sum(pair_sum, row_dim, wire_type):
    arrived = lax.all_to_all(pair_sum.astype(wire_type), CHIPS, row_dim, row_dim, tiled=True)
    return jnp.sum(arrived.astype(jnp.float32), axis=row_dim)


def gathered_rows_wide(shard):
    chips = lax.axis_size(CHIPS)
    from_chips = lax.all_to_all(
        jnp.broadcast_to(shard[None], (chips, *shard.shape)), CHIPS, 0, 0, tiled=True
    )
    from_partner = swap_cores(from_chips)
    first = lax.axis_index(CORES) == 0
    low_core = jnp.where(first, from_chips, from_partner)
    high_core = jnp.where(first, from_partner, from_chips)
    return jnp.stack([low_core, high_core], axis=1).reshape(-1, *shard.shape[1:])


def copy_for_each(shard, axis):
    length = axis_length(axis)
    return lax.all_to_all(
        jnp.broadcast_to(shard[None], (length, *shard.shape)), axis, 0, 0, tiled=True
    )


def of_everyone(shard, axis):
    return copy_for_each(shard, axis).sum(axis=0)


def laid_out(parts, dim):
    parts = jnp.moveaxis(parts, 0, dim)
    lengths = parts.shape
    return parts.reshape(*lengths[:dim], lengths[dim] * lengths[dim + 1], *lengths[dim + 2 :])


def gathered_copies(shard, axis, dim):
    parts = copy_for_each(shard, axis)
    return laid_out(parts, dim)


def in_blocks(shard, dim, length):
    before, after = (shard.shape[:dim], shard.shape[dim + 1 :])
    return jnp.moveaxis(shard.reshape(*before, length, -1, *after), dim, 0)


def summed_on_arrival(shard, axis, dim):
    parts = in_blocks(shard, dim, axis_length(axis))
    arrived = lax.all_to_all(parts, axis, split_axis=0, concat_axis=0, tiled=True)
    return arrived.sum(axis=0)


def sent_and_summed(shard, axis, dim):
    length = axis_length(axis)
    parts = lax.all_to_all(in_blocks(shard, dim, length), axis, 0, 0, tiled=True)
    return jnp.sum(parts.astype(jnp.float32), axis=0)


def scale_rows(floats, square_sum, gain):
    scaled = (
        floats * lax.rsqrt(square_sum / D + EPSILON)[:, None] * gain.astype(jnp.float32)[None, :]
    )
    return scaled.astype(jnp.bfloat16)


def norm_rows(stream, gain):
    floats = stream.astype(jnp.float32)
    square_sum = of_everyone(jnp.sum(floats * floats, axis=1), WIDE)
    return gathered_copies(scale_rows(floats, square_sum, gain), "narrow", 0)


def rotate_pairs(vectors, cosine, sine_table):
    half_dim = vectors.shape[-1] // 2
    first_half = vectors[..., :half_dim]
    second_half = vectors[..., half_dim:]
    return jnp.concatenate(
        [
            first_half * cosine - second_half * sine_table,
            second_half * cosine + first_half * sine_table,
        ],
        axis=-1,
    )


def rotary_tables(lengths, head_dim):
    half_dim = head_dim // 2
    inverse = jnp.exp(
        jnp.arange(half_dim, dtype=jnp.float32) * (-2.0 * math.log(ROPE_BASE) / head_dim)
    )
    angles = lengths.astype(jnp.float32)[:, None] * inverse[None, :]
    return (jnp.cos(angles), jnp.sin(angles))


def split_heads(projected, lengths, heads_kv, head_dim):
    row_count = projected.shape[0]
    grouped = projected.reshape(row_count, heads_kv, -1, head_dim)
    group_size = grouped.shape[2] - 2
    cosine, sine_table = rotary_tables(lengths, head_dim)
    rotated = rotate_pairs(
        grouped[:, :, : group_size + 1], cosine[:, None, None, :], sine_table[:, None, None, :]
    )
    queries = rotated[:, :, :group_size].astype(jnp.bfloat16)
    key_new = rotated[:, :, group_size].astype(jnp.bfloat16)
    value_new = grouped[:, :, group_size + 1].astype(jnp.bfloat16)
    return (queries, key_new, value_new)


def attend(queries, key_new, value_new, cached_keys, cached_values, lengths):
    row_count, heads_kv, group_size, head_dim = queries.shape
    slot_count = cached_keys.shape[0]
    score_scale = 1.0 / math.sqrt(head_dim)
    key_table = cached_keys.reshape(slot_count, heads_kv, head_dim)
    value_table = cached_values.reshape(slot_count, heads_kv, head_dim)
    starts = jnp.cumsum(lengths) - lengths
    position = jnp.arange(slot_count, dtype=jnp.int32)
    owned = (position[None, :] >= starts[:, None]) & (
        position[None, :] < (starts + lengths)[:, None]
    )
    scores = (
        jnp.einsum("rkgd,tkd->krgt", queries, key_table, preferred_element_type=jnp.float32)
        * score_scale
    )
    scores = jnp.where(owned[None, :, None, :], scores, -jnp.inf)
    own_score = (
        jnp.einsum("rkgd,rkd->krg", queries, key_new, preferred_element_type=jnp.float32)
        * score_scale
    )
    row_peak = jnp.maximum(jnp.max(scores, axis=3), own_score)
    weights = jnp.exp(scores - row_peak[..., None])
    own_weight = jnp.exp(own_score - row_peak)
    weight_sum = jnp.sum(weights, axis=3) + own_weight
    blended = jnp.einsum(
        "krgt,tkd->krgd",
        weights.astype(jnp.bfloat16),
        value_table,
        preferred_element_type=jnp.float32,
    )
    own_rounded = lax.optimization_barrier(own_weight.astype(jnp.bfloat16)).astype(jnp.float32)
    blended = blended + own_rounded[..., None] * jnp.transpose(value_new, (1, 0, 2))[
        :, :, None, :
    ].astype(jnp.float32)
    normalized = (blended / weight_sum[..., None]).astype(jnp.bfloat16)
    return jnp.transpose(normalized, (1, 0, 2, 3)).reshape(
        row_count, heads_kv * group_size * head_dim
    )


def split_hi_lo(values):
    high = values.astype(jnp.bfloat16)
    low = (values - high.astype(jnp.float32)).astype(jnp.bfloat16)
    return high, low


def gathered_rows(stream, gain):
    floats = stream.astype(jnp.float32)
    square_sum = jnp.sum(floats * floats, axis=1)
    scaled = (floats * gain.astype(jnp.float32)[None, :]).astype(jnp.bfloat16)
    high, low = split_hi_lo(square_sum)
    packed = jnp.concatenate([scaled, high[:, None], low[:, None]], axis=1)
    rows = gathered_copies(packed, "narrow", 0)
    width = stream.shape[1]
    partial_sum = rows[:, width].astype(jnp.float32) + rows[:, width + 1].astype(jnp.float32)
    return rows[:, :width], partial_sum


def row_scale(square_sum):
    return lax.rsqrt(square_sum / D + EPSILON)


def on_device(
    hidden_in, lengths, kv_cache, qkv_weight, o_weight, gate_up, down_weight, attn_gain, mlp_gain
):
    width_dev = hidden_in.shape[1]
    heads_kv = qkv_weight.shape[1]
    hidden_dev = down_weight.shape[0]
    flat_qkv = qkv_weight.reshape(width_dev, -1)
    stream = hidden_in
    entries = []
    for layer_index in range(LAYERS):
        if layer_index == 0:
            rows_in = norm_rows(stream, attn_gain)
            pair_sum, row_dim = reduced_rows(
                jnp.dot(rows_in, flat_qkv, preferred_element_type=jnp.float32), 0, jnp.float32
            )
            own_qkv = chip_sum(pair_sum, row_dim, jnp.float32)
        else:
            rows_in, partial_sum = gathered_rows(stream, attn_gain)
            projected = jnp.dot(rows_in, flat_qkv, preferred_element_type=jnp.float32)
            pair_sum, row_dim = reduced_rows(
                jnp.concatenate([projected, partial_sum[:, None]], axis=1), 0, jnp.float32
            )
            own = chip_sum(pair_sum, row_dim, jnp.float32)
            qkv_cols = flat_qkv.shape[1]
            own_qkv = own[:, :qkv_cols] * row_scale(own[:, qkv_cols])[:, None]
        queries, key_new, value_new = split_heads(own_qkv, lengths, heads_kv, HD)
        own_rows = key_new.shape[0]
        entries.append(
            jnp.stack(
                [
                    key_new.reshape(own_rows, heads_kv * HD),
                    value_new.reshape(own_rows, heads_kv * HD),
                ]
            )
        )
        attended = attend(
            queries, key_new, value_new, kv_cache[layer_index, 0], kv_cache[layer_index, 1], lengths
        )
        heads_all = gathered_copies(attended, WIDE, 0)
        summed = summed_on_arrival(
            jnp.dot(heads_all, o_weight, preferred_element_type=jnp.float32), "narrow", 0
        )
        stream = (stream.astype(jnp.float32) + summed).astype(jnp.bfloat16)
        rows_in, partial_sum = gathered_rows(stream, mlp_gain)
        chips = lax.axis_size(CHIPS)
        core = lax.axis_index(CORES)
        by_core = rows_in.reshape(chips, 2, -1, rows_in.shape[1])
        sums_by_core = partial_sum.reshape(chips, 2, -1)
        reordered = jnp.concatenate(
            [
                lax.dynamic_index_in_dim(by_core, 1 - core, 1, keepdims=False),
                lax.dynamic_index_in_dim(by_core, core, 1, keepdims=False),
            ]
        ).reshape(rows_in.shape)
        reordered_sums = jnp.concatenate(
            [
                lax.dynamic_index_in_dim(sums_by_core, 1 - core, 1, keepdims=False),
                lax.dynamic_index_in_dim(sums_by_core, core, 1, keepdims=False),
            ]
        ).reshape(partial_sum.shape)
        both_parts = jnp.einsum(
            "rd,dkh->krh", reordered, gate_up, preferred_element_type=jnp.float32
        ).astype(jnp.bfloat16)
        high, low = split_hi_lo(reordered_sums)
        sums_col = jnp.stack([high, low])[:, :, None]
        payload = jnp.concatenate([both_parts, sums_col], axis=2)
        half = payload.shape[1] // 2
        block_shape = (2, chips, half // chips, hidden_dev + 1)
        to_partner = payload[:, :half].reshape(block_shape)
        kept = payload[:, half:].reshape(block_shape)
        from_partner = swap_cores(to_partner)
        pair_squares = (
            kept[0, :, :, hidden_dev].astype(jnp.float32)
            + kept[1, :, :, hidden_dev].astype(jnp.float32)
            + from_partner[0, :, :, hidden_dev].astype(jnp.float32)
            + from_partner[1, :, :, hidden_dev].astype(jnp.float32)
        )
        high, low = split_hi_lo(pair_squares)
        resplit = jnp.stack([high, low]).astype(jnp.float32)[..., None]
        column = lax.broadcasted_iota(jnp.int32, block_shape, 3)
        pair_sum = jnp.where(
            column == hidden_dev,
            resplit,
            kept.astype(jnp.float32) + from_partner.astype(jnp.float32),
        ).astype(jnp.bfloat16)
        own = chip_sum(pair_sum, 1, jnp.bfloat16)
        scale = row_scale(own[0, :, hidden_dev] + own[1, :, hidden_dev])[:, None]
        gate = own[0, :, :hidden_dev] * scale
        up = own[1, :, :hidden_dev] * scale
        activated = (jax.nn.silu(gate) * up).astype(jnp.bfloat16)
        partial_down = jnp.dot(
            gathered_rows_wide(activated), down_weight, preferred_element_type=jnp.float32
        )
        summed = summed_on_arrival(partial_down, "narrow", 0)
        stream = (stream.astype(jnp.float32) + summed).astype(jnp.bfloat16)
    return (stream, jnp.stack(entries))


def solution(mesh):
    wide_size, narrow_size = mesh.devices.shape
    split_mesh = Mesh(
        mesh.devices.reshape(wide_size // 2, 2, narrow_size), (CHIPS, CORES, "narrow")
    )
    return jax.shard_map(
        on_device,
        mesh=split_mesh,
        in_specs=(
            P("narrow", WIDE),
            P(WIDE),
            P(None, None, WIDE, "narrow"),
            P(WIDE, "narrow", None),
            P("narrow", WIDE),
            P(WIDE, None, "narrow"),
            P("narrow", WIDE),
            P(WIDE),
            P(WIDE),
        ),
        out_specs=(P("narrow", WIDE), P(None, None, WIDE, "narrow")),
        check_vma=False,
    )
```
